128 devices in a mesh: ctx: 32 (over z, y, core), head: 4 (over x).
Axes of the slice: x: 4, y: 4, z: 4, core: 2. Of those that a mesh axis runs over, the one named last changes fastest.
Arguments:
- tokens: bfloat16 [12288, 3840], P(('ctx', 'head'))
- w_query: bfloat16 [3840, 4096], P(None, 'head')
- w_key: bfloat16 [3840, 2048], P(None, 'head')
- w_value: bfloat16 [3840, 2048], P(None, 'head'), may hold values from -0.09375 to 0.09375
- query_gain: float32 [256], replicated
- key_gain: float32 [256], replicated
- positions: int32 [12288], P('ctx'), may hold values from 0 to 3071, as said below
- out_grad: bfloat16 [12288, 4096], P('ctx', 'head'), may hold values from -6 to 6
Outputs:
- attended: bfloat16 [12288, 4096], P('ctx', 'head')
- input_grad: bfloat16 [12288, 3840], P(('ctx', 'head'))
- grad_query: bfloat16 [3840, 4096], P('ctx', 'head')
- grad_key: bfloat16 [3840, 2048], P('ctx', 'head')
- grad_value: bfloat16 [3840, 2048], P('ctx', 'head')
The draws below stay inside these ranges and needn't reach their ends.
Inputs may be any that keep to these rules, and one draw needn't show every extreme that they name: `positions`: positions rise by one from token to token inside a document and are 0 at a document's first token; the window's first document began before the window; no document that starts inside the window is longer than 2048 tokens.
All inputs are finite; a program needn't handle non-finite values.
Results may differ from the reference program's by a relative error of at most 0.04.
The reference program's roundings to bfloat16 on the way count: a program that leaves them out, or rounds other values in their place, can miss the bound.
Values may be sent and summed in bfloat16 or wider, within the bound.
No kernel may reach another device: no remote copies, remote signals or barrier semaphores. Data moves between devices by JAX's collectives and lax.ppermute only.
A program may use at most 192 MiB of HBM per device.

```python
import math
import jax
import jax.numpy as jnp
from jax import lax

D = 3840
HEADS = 16
KV_HEADS = 8
HEAD_DIM = 256
WINDOW = 1024
TOK_DEV = 384
TOKENS = 12288
REACH = 3
PROJ = 8192
N_CTX = 32


def draw_tokens(key, part):
    draws = jnp.clip(jax.random.normal(jax.random.fold_in(key, 3), (TOKENS, D), jnp.float32), -6.0, 6.0)
    return draws.astype(jnp.bfloat16)


def draw_w_query(key, part):
    random_part = jax.random.normal(jax.random.fold_in(key, 1), (D, HEADS, HEAD_DIM), jnp.float32)
    return (random_part / jnp.sqrt(float(D))).reshape(D, HEADS * HEAD_DIM).astype(jnp.bfloat16)


def draw_w_key(key, part):
    random_part = jax.random.normal(jax.random.fold_in(key, 2), (D, KV_HEADS, HEAD_DIM), jnp.float32)
    return (random_part / jnp.sqrt(float(D))).reshape(D, KV_HEADS * HEAD_DIM).astype(jnp.bfloat16)


def draw_query_gain(key, part):
    return jnp.exp(jax.random.uniform(jax.random.fold_in(key, 21), (HEAD_DIM,), jnp.float32, 0.0, 0.92))


def draw_key_gain(key, part):
    return jnp.exp(jax.random.uniform(jax.random.fold_in(key, 22), (HEAD_DIM,), jnp.float32, 0.0, 0.92))


def draw_positions(key, part):
    token_index = jnp.arange(TOKENS, dtype=jnp.int32)
    random_start = jax.random.randint(jax.random.fold_in(key, 5), (TOKENS,), 0, WINDOW) == 0
    after_first = token_index - WINDOW
    forced_start = (after_first >= 0) & (after_first % (2 * WINDOW) == 0)
    boundary = forced_start | random_start & (after_first > 0)
    last_start = lax.cummax(jnp.where(boundary, token_index, -2 * WINDOW), axis=0)
    return (token_index - last_start).astype(jnp.int32)


def level_of(stream_key, extent, pieces, least, largest):
    loudness, own = 1.0, jax.random.fold_in(stream_key, 6)
    for dim, shards_of in pieces:
        steps = jnp.exp(jax.random.uniform(jax.random.fold_in(own, dim), (shards_of,), jnp.float32, least / len(pieces), largest / len(pieces)))
        loudness = loudness * jnp.repeat(steps, extent[dim] // shards_of).reshape([-1 if axis == dim else 1 for axis in range(len(extent))])
    return loudness


def bell_draw(key, dims, spread, bound, cuts=(), held_as=jnp.bfloat16):
    result = jax.random.normal(key, dims, jnp.float32) * spread
    if len(cuts) > 0:
        result = level_of(key, dims, cuts, -0.22, 0.18) * result
    return jnp.clip(result, min=-bound, max=bound).astype(held_as)


def setup_inputs(seed: int = 0) -> dict:
    streams_of = jax.random.split(jax.random.key(seed), 9)
    tokens = draw_tokens(jax.random.fold_in(streams_of[8], 71), 0)
    w_query = draw_w_query(jax.random.fold_in(streams_of[8], 71), 0)
    w_key = draw_w_key(jax.random.fold_in(streams_of[8], 71), 0)
    w_value = bell_draw(streams_of[3], (D, KV_HEADS * HEAD_DIM), D ** -0.5, 0.09375, ((1, 4),))
    query_gain = draw_query_gain(jax.random.fold_in(streams_of[8], 71), 0)
    key_gain = draw_key_gain(jax.random.fold_in(streams_of[8], 71), 0)
    positions = draw_positions(jax.random.fold_in(streams_of[8], 71), 0)
    out_grad = bell_draw(streams_of[7], (TOKENS, HEADS * HEAD_DIM), 1.0, 6.0, ((0, 32), (1, 4)))
    return {"tokens": tokens, "w_query": w_query, "w_key": w_key, "w_value": w_value, "query_gain": query_gain, "key_gain": key_gain, "positions": positions, "out_grad": out_grad}


norm_eps = 1e-06
rope_base = 10000.0

def rope_tables(positions, head_width):
    half_width = head_width // 2
    indices = jnp.arange(half_width, dtype=jnp.float32)
    frequency = jnp.power(rope_base, -2.0 * indices / head_width)
    angles = positions.astype(jnp.float32)[:, None] * frequency[None, :]
    return (jnp.cos(angles)[:, None, :], jnp.sin(angles)[:, None, :])

def rotate(vector, cosine_table, sine_table):
    half_width = vector.shape[-1] // 2
    lower_half = vector[..., :half_width]
    upper_half = vector[..., half_width:]
    return jnp.concatenate([lower_half * cosine_table - upper_half * sine_table, upper_half * cosine_table + lower_half * sine_table], axis=-1)

def unrotate(rotated, cosine_table, sine_table):
    half_width = rotated.shape[-1] // 2
    lower_half = rotated[..., :half_width]
    upper_half = rotated[..., half_width:]
    return jnp.concatenate([lower_half * cosine_table + upper_half * sine_table, upper_half * cosine_table - lower_half * sine_table], axis=-1)

def normalize(vector, gain_vector):
    inv_rms = lax.rsqrt(lax.optimization_barrier(jnp.mean(vector * vector, axis=-1, keepdims=True)) + norm_eps)
    return (vector * inv_rms * gain_vector, inv_rms)

def norm_back(vector, inv_rms, gain_vector, upstream):
    scaled = upstream * gain_vector
    return inv_rms * scaled - vector * (inv_rms * inv_rms * inv_rms) * lax.optimization_barrier(jnp.mean(vector * scaled, axis=-1, keepdims=True))

def through_bf16(vector):
    return lax.optimization_barrier(vector.astype(jnp.bfloat16)).astype(jnp.float32)

def reference(tokens, w_query, w_key, w_value, query_gain, key_gain, positions, out_grad):
    group_size = HEADS // KV_HEADS
    query_scale = 1.0 / math.sqrt(HEAD_DIM)
    query_raw = jnp.dot(tokens, w_query, preferred_element_type=jnp.float32).reshape(TOKENS, HEADS, HEAD_DIM)
    key_raw = jnp.dot(tokens, w_key, preferred_element_type=jnp.float32).reshape(TOKENS, KV_HEADS, HEAD_DIM)
    value_states = jnp.dot(tokens, w_value, preferred_element_type=jnp.float32).astype(jnp.bfloat16).reshape(TOKENS, KV_HEADS, HEAD_DIM)
    cosine_table, sine_table = rope_tables(positions, HEAD_DIM)
    query_normed, query_inv = normalize(query_raw, query_gain)
    key_normed, key_inv = normalize(key_raw, key_gain)
    query_states = (rotate(query_normed, cosine_table, sine_table) * query_scale).astype(jnp.bfloat16)
    key_states = rotate(key_normed, cosine_table, sine_table).astype(jnp.bfloat16)
    pad_rows = REACH * TOK_DEV
    key_span = (REACH + 1) * TOK_DEV
    key_padded = jnp.concatenate([jnp.zeros((pad_rows, KV_HEADS, HEAD_DIM), jnp.bfloat16), key_states], axis=0)
    value_padded = jnp.concatenate([jnp.zeros((pad_rows, KV_HEADS, HEAD_DIM), jnp.bfloat16), value_states], axis=0)
    query_blocks = query_states.reshape(N_CTX, TOK_DEV, KV_HEADS, group_size, HEAD_DIM)
    grad_blocks = out_grad.reshape(N_CTX, TOK_DEV, KV_HEADS, group_size, HEAD_DIM)
    position_blocks = positions.reshape(N_CTX, TOK_DEV)
    query_offsets = jnp.arange(TOK_DEV, dtype=jnp.int32)
    key_offsets = jnp.arange(key_span, dtype=jnp.int32)

    def attend_block(accumulated, operands):
        key_grad_sum, value_grad_sum = accumulated
        block_index, query_block, grad_block, position_block = operands
        first_row = block_index * TOK_DEV
        key_block = lax.dynamic_slice_in_dim(key_padded, first_row, key_span, 0).astype(jnp.float32)
        value_block = lax.dynamic_slice_in_dim(value_padded, first_row, key_span, 0).astype(jnp.float32)
        query_index = first_row + query_offsets
        key_index = first_row - pad_rows + key_offsets
        distance = query_index[:, None] - key_index[None, :]
        reach_limit = jnp.minimum(position_block, WINDOW - 1)[:, None]
        visible = (distance >= 0) & (distance <= reach_limit) & (key_index[None, :] >= 0)
        query_float = query_block.astype(jnp.float32)
        grad_float = grad_block.astype(jnp.float32)
        scores = jnp.einsum('qgue,kge->guqk', query_float, key_block)
        row_peak = lax.optimization_barrier(jnp.max(jnp.where(visible, scores, -jnp.inf), axis=-1, keepdims=True))
        weights = jnp.where(visible, jnp.exp(scores - row_peak), 0.0)
        probabilities = weights / lax.optimization_barrier(jnp.sum(weights, axis=-1, keepdims=True))
        prob_float = through_bf16(probabilities)
        attended = jnp.einsum('guqk,kge->qgue', prob_float, value_block)
        attended_bf = attended.astype(jnp.bfloat16)
        attended_float = lax.optimization_barrier(attended_bf).astype(jnp.float32)
        row_delta = jnp.einsum('qgue,qgue->guq', grad_float, attended_float)[..., None]
        dprobs = jnp.einsum('qgue,kge->guqk', grad_float, value_block)
        dscores = through_bf16(probabilities * (dprobs - row_delta))
        query_grad = jnp.einsum('guqk,kge->qgue', dscores, key_block)
        key_grad = jnp.einsum('guqk,qgue->kge', dscores, query_float)
        value_grad = jnp.einsum('guqk,qgue->kge', prob_float, grad_float)
        key_grad_sum = lax.dynamic_update_slice_in_dim(key_grad_sum, lax.dynamic_slice_in_dim(key_grad_sum, first_row, key_span, 0) + key_grad, first_row, 0)
        value_grad_sum = lax.dynamic_update_slice_in_dim(value_grad_sum, lax.dynamic_slice_in_dim(value_grad_sum, first_row, key_span, 0) + value_grad, first_row, 0)
        return ((key_grad_sum, value_grad_sum), (attended_bf, query_grad))
    zero_sum = jnp.zeros((pad_rows + TOKENS, KV_HEADS, HEAD_DIM), jnp.float32)
    block_ids = jnp.arange(N_CTX, dtype=jnp.int32)
    sums, outputs = lax.scan(attend_block, (zero_sum, zero_sum), (block_ids, query_blocks, grad_blocks, position_blocks))
    key_grad_sum, value_grad_sum = sums
    attended_blocks, query_grad_blocks = outputs
    attended = attended_blocks.reshape(TOKENS, HEADS * HEAD_DIM)
    query_grads = query_grad_blocks.reshape(TOKENS, HEADS, HEAD_DIM)
    key_grads = key_grad_sum[pad_rows:]
    value_grads = value_grad_sum[pad_rows:].astype(jnp.bfloat16).reshape(TOKENS, KV_HEADS * HEAD_DIM)
    query_raw_grad = norm_back(query_raw, query_inv, query_gain, unrotate(query_grads, cosine_table, sine_table) * query_scale).astype(jnp.bfloat16).reshape(TOKENS, HEADS * HEAD_DIM)
    key_raw_grad = norm_back(key_raw, key_inv, key_gain, unrotate(key_grads, cosine_table, sine_table)).astype(jnp.bfloat16).reshape(TOKENS, KV_HEADS * HEAD_DIM)
    input_grad = (jnp.dot(query_raw_grad, w_query.T, preferred_element_type=jnp.float32) + jnp.dot(key_raw_grad, w_key.T, preferred_element_type=jnp.float32) + jnp.dot(value_grads, w_value.T, preferred_element_type=jnp.float32)).astype(jnp.bfloat16)
    grad_columns = jnp.concatenate([query_raw_grad, key_raw_grad, value_grads], axis=1)
    token_blocks = tokens.reshape(N_CTX, TOK_DEV, D)
    column_blocks = grad_columns.reshape(N_CTX, TOK_DEV, PROJ)

    def add_term(weight_sum, operands):
        block_term = jnp.dot(operands[0].T, operands[1], preferred_element_type=jnp.float32)
        return (weight_sum + through_bf16(block_term), None)
    weight_sum, unused = lax.scan(add_term, jnp.zeros((D, PROJ), jnp.float32), (token_blocks, column_blocks))
    query_cols = HEADS * HEAD_DIM
    key_cols = KV_HEADS * HEAD_DIM
    grad_query = weight_sum[:, :query_cols].astype(jnp.bfloat16)
    grad_key = weight_sum[:, query_cols:query_cols + key_cols].astype(jnp.bfloat16)
    grad_value = weight_sum[:, query_cols + key_cols:].astype(jnp.bfloat16)
    return (attended, input_grad, grad_query, grad_key, grad_value)
```

```python
from functools import reduce
import math

import jax
import jax.numpy as jnp
from jax import lax
from jax.sharding import PartitionSpec as P

WINDOW = 1024


norm_eps = 1e-06
rope_base = 10000.0


def passed_along(block, axis, distance):
    devices = range(lax.axis_size(axis))
    route = [(i - distance, i) for i in devices if i - distance in devices]
    return lax.ppermute(block, axis, route)


CORES = 2
Y_CHIPS = 4


def ring_pairs(rank_count, along_y):
    z_chips = rank_count // (CORES * Y_CHIPS)
    forward = []
    for z in range(z_chips):
        for y in range(Y_CHIPS):
            for core in range(CORES):
                source = (z * Y_CHIPS + y) * CORES + core
                if along_y:
                    target = (z * Y_CHIPS + (y + 1) % Y_CHIPS) * CORES + core
                else:
                    target = (((z + 1) % z_chips) * Y_CHIPS + y) * CORES + core
                forward.append((source, target))
    backward = [(target, source) for source, target in forward]
    return forward, backward


def ring_reduce_scatter(parts, axis, position, forward, backward):
    count = parts.shape[axis]
    half = parts.shape[-1] // 2

    def own(index, low):
        piece = lax.slice_in_dim(parts, low, low + half, axis=parts.ndim - 1)
        return lax.dynamic_index_in_dim(piece, index % count, axis, keepdims=False)

    up = own(position + count - 1, 0)
    down = own(position + 1, half)
    for step in range(count - 1):
        up = lax.ppermute(up.astype(jnp.bfloat16), "ctx", forward).astype(jnp.float32) + own(
            position + 2 * count - step - 2, 0
        )
        down = lax.ppermute(down.astype(jnp.bfloat16), "ctx", backward).astype(
            jnp.float32
        ) + own(position + step + 2, half)
    return jnp.concatenate([up, down], axis=-1)


def torus_reduce_scatter(partial, my_rank, rank_count):
    z_chips = rank_count // (CORES * Y_CHIPS)
    rows, columns = partial.shape
    per_rank = rows // rank_count
    core = my_rank % CORES
    y_pos = (my_rank // CORES) % Y_CHIPS
    z_pos = my_rank // (CORES * Y_CHIPS)
    grid = partial.reshape(z_chips, Y_CHIPS, CORES, per_rank, columns)
    mine = lax.dynamic_index_in_dim(grid, core, 2, keepdims=False)
    other = lax.dynamic_index_in_dim(grid, CORES - 1 - core, 2, keepdims=False)
    partner = [(rank, rank ^ 1) for rank in range(rank_count)]
    pair_sum = mine + lax.ppermute(other.astype(jnp.bfloat16), "ctx", partner).astype(jnp.float32)
    y_forward, y_backward = ring_pairs(rank_count, True)
    z_forward, z_backward = ring_pairs(rank_count, False)
    half = columns // 2
    first = pair_sum[..., :half]
    second = pair_sum[..., half:]
    first = ring_reduce_scatter(first, 1, y_pos, y_forward, y_backward)
    first = ring_reduce_scatter(first, 0, z_pos, z_forward, z_backward)
    second = ring_reduce_scatter(second, 0, z_pos, z_forward, z_backward)
    second = ring_reduce_scatter(second, 0, y_pos, y_forward, y_backward)
    return jnp.concatenate([first, second], axis=-1)


def rope_tables(positions, head_width):
    half_width = head_width // 2
    indices = jnp.arange(half_width, dtype=jnp.float32)
    frequency = jnp.power(rope_base, -2.0 * indices / head_width)
    angles = positions.astype(jnp.float32)[:, None] * frequency[None, :]
    return (jnp.cos(angles)[:, None, :], jnp.sin(angles)[:, None, :])


def rotate(vector, cosine_table, sine_table):
    half_width = vector.shape[-1] // 2
    lower_half = vector[..., :half_width]
    upper_half = vector[..., half_width:]
    return jnp.concatenate(
        [
            lower_half * cosine_table - upper_half * sine_table,
            upper_half * cosine_table + lower_half * sine_table,
        ],
        axis=-1,
    )


def unrotate(rotated, cosine_table, sine_table):
    half_width = rotated.shape[-1] // 2
    lower_half = rotated[..., :half_width]
    upper_half = rotated[..., half_width:]
    return jnp.concatenate(
        [
            lower_half * cosine_table + upper_half * sine_table,
            upper_half * cosine_table - lower_half * sine_table,
        ],
        axis=-1,
    )


def normalize(vector, gain_vector):
    inv_rms = lax.rsqrt(jnp.mean(vector * vector, axis=-1, keepdims=True) + norm_eps)
    return (vector * inv_rms * gain_vector, inv_rms)


def norm_back(vector, inv_rms, gain_vector, upstream):
    scaled = upstream * gain_vector
    return inv_rms * scaled - vector * (inv_rms * inv_rms * inv_rms) * jnp.mean(
        vector * scaled, axis=-1, keepdims=True
    )


def on_device(tokens, w_query, w_key, w_value, query_gain, key_gain, positions, out_grad):
    gathered = lax.all_gather(tokens, "head", axis=0, tiled=True)
    row_count = gathered.shape[0]
    head_width = query_gain.shape[0]
    head_count = w_query.shape[1] // head_width
    groups = w_key.shape[1] // head_width
    group_size = head_count // groups
    rank_count = lax.axis_size("ctx")
    my_rank = lax.axis_index("ctx")
    reach_blocks = min((WINDOW - 2) // row_count + 1, rank_count - 1)
    query_scale = 1.0 / math.sqrt(head_width)
    query_raw = jnp.dot(gathered, w_query, preferred_element_type=jnp.float32).reshape(
        row_count, head_count, head_width
    )
    key_raw = jnp.dot(gathered, w_key, preferred_element_type=jnp.float32).reshape(
        row_count, groups, head_width
    )
    value_states = jnp.dot(gathered, w_value, preferred_element_type=jnp.float32).astype(
        jnp.bfloat16
    )
    cosine_table, sine_table = rope_tables(positions, head_width)
    query_normed, query_inv = normalize(query_raw, query_gain)
    key_normed, key_inv = normalize(key_raw, key_gain)
    query_states = (
        (rotate(query_normed, cosine_table, sine_table) * query_scale)
        .astype(jnp.bfloat16)
        .reshape(row_count, groups, group_size, head_width)
    )
    key_states = (
        rotate(key_normed, cosine_table, sine_table)
        .astype(jnp.bfloat16)
        .reshape(row_count, groups * head_width)
    )
    local_kv = jnp.stack([key_states, value_states])
    blocks = [local_kv]
    moving = local_kv
    for stride in range(reach_blocks):
        moving = passed_along(moving, "ctx", 1)
        blocks.append(moving)
    offsets = jnp.arange(row_count, dtype=jnp.int32)
    reach_limit = jnp.minimum(positions, WINDOW - 1)[:, None]
    visible_sets = []
    live_flags = []
    for stride in range(reach_blocks + 1):
        distance = stride * row_count + offsets[:, None] - offsets[None, :]
        visible = (distance >= 0) & (distance <= reach_limit) & (my_rank >= stride)
        visible_sets.append(visible)
        live_flags.append(jnp.any(visible))

    def block_keys(stride):
        return blocks[stride][0].reshape(row_count, groups, head_width)

    def block_values(stride):
        return blocks[stride][1].reshape(row_count, groups, head_width)

    def score_block(stride):
        return jnp.einsum(
            "qgue,kge->guqk", query_states, block_keys(stride), preferred_element_type=jnp.float32
        )

    scores = [score_block(stride) for stride in range(reach_blocks + 1)]
    row_peak = reduce(
        jnp.maximum,
        [
            jnp.max(
                jnp.where(visible_sets[stride], scores[stride], -jnp.inf), axis=-1, keepdims=True
            )
            for stride in range(reach_blocks + 1)
        ],
    )
    weights = [
        jnp.where(visible_sets[stride], jnp.exp(scores[stride] - row_peak), 0.0)
        for stride in range(reach_blocks + 1)
    ]
    row_total = reduce(
        jnp.add, [jnp.sum(weight_block, axis=-1, keepdims=True) for weight_block in weights]
    )
    probabilities = [weight_block / row_total for weight_block in weights]
    prob_bf16 = [prob_block.astype(jnp.bfloat16) for prob_block in probabilities]

    def mix_values(stride):
        return jnp.einsum(
            "guqk,kge->qgue",
            prob_bf16[stride],
            block_values(stride),
            preferred_element_type=jnp.float32,
        )

    mixed = reduce(jnp.add, [mix_values(stride) for stride in range(reach_blocks + 1)])
    attended = mixed.astype(jnp.bfloat16)
    grad_heads = out_grad.reshape(row_count, groups, group_size, head_width)
    row_delta = jnp.einsum(
        "qgue,qgue->guq", grad_heads, attended, preferred_element_type=jnp.float32
    )[..., None]

    def back_block(stride):
        key_block = block_keys(stride)
        dprobs = jnp.einsum(
            "qgue,kge->guqk", grad_heads, block_values(stride), preferred_element_type=jnp.float32
        )
        dscores = (probabilities[stride] * (dprobs - row_delta)).astype(jnp.bfloat16)
        query_grad = jnp.einsum(
            "guqk,kge->qgue", dscores, key_block, preferred_element_type=jnp.float32
        )
        key_grad = jnp.einsum(
            "guqk,qgue->kge", dscores, query_states, preferred_element_type=jnp.float32
        )
        value_grad = jnp.einsum(
            "guqk,qgue->kge", prob_bf16[stride], grad_heads, preferred_element_type=jnp.float32
        )
        return (
            query_grad,
            jnp.stack(
                [
                    key_grad.reshape(row_count, groups * head_width),
                    value_grad.reshape(row_count, groups * head_width),
                ]
            ),
        )

    back_terms = [back_block(stride) for stride in range(reach_blocks + 1)]
    query_grads = reduce(jnp.add, [term_pair[0] for term_pair in back_terms])
    key_grad_parts = [term_pair[1] for term_pair in back_terms]
    returned = key_grad_parts[reach_blocks]
    for stride in range(reach_blocks, 0, -1):
        returned = (
            passed_along(returned.astype(jnp.bfloat16), "ctx", -1).astype(returned.dtype)
            + key_grad_parts[stride - 1]
        )
    key_grads = returned[0].reshape(row_count, groups, head_width)
    value_grads = returned[1].astype(jnp.bfloat16)
    query_raw_grad = (
        norm_back(
            query_raw,
            query_inv,
            query_gain,
            unrotate(
                query_grads.reshape(row_count, head_count, head_width), cosine_table, sine_table
            )
            * query_scale,
        )
        .astype(jnp.bfloat16)
        .reshape(row_count, head_count * head_width)
    )
    key_raw_grad = (
        norm_back(key_raw, key_inv, key_gain, unrotate(key_grads, cosine_table, sine_table))
        .astype(jnp.bfloat16)
        .reshape(row_count, groups * head_width)
    )
    input_terms = (
        jnp.dot(query_raw_grad, w_query.T, preferred_element_type=jnp.float32)
        + jnp.dot(key_raw_grad, w_key.T, preferred_element_type=jnp.float32)
        + jnp.dot(value_grads, w_value.T, preferred_element_type=jnp.float32)
    )
    input_grad = lax.psum_scatter(
        input_terms.astype(jnp.bfloat16), "head", scatter_dimension=0, tiled=True
    )
    grad_columns = jnp.concatenate([query_raw_grad, key_raw_grad, value_grads], axis=1)
    block_term = (
        lax.dot_general(
            gathered, grad_columns, (((0,), (0,)), ((), ())), preferred_element_type=jnp.float32
        )
        .astype(jnp.bfloat16)
        .astype(jnp.float32)
    )
    summed = torus_reduce_scatter(block_term, my_rank, rank_count).astype(jnp.bfloat16)
    query_cols = head_count * head_width
    key_cols = groups * head_width
    return (
        attended.reshape(row_count, query_cols),
        input_grad,
        summed[:, :query_cols],
        summed[:, query_cols : query_cols + key_cols],
        summed[:, query_cols + key_cols :],
    )


def solution(mesh):
    in_specs = (
        P(("ctx", "head"), None),
        P(None, "head"),
        P(None, "head"),
        P(None, "head"),
        P(),
        P(),
        P("ctx"),
        P("ctx", "head"),
    )
    out_specs = (
        P("ctx", "head"),
        P(("ctx", "head"), None),
        P("ctx", "head"),
        P("ctx", "head"),
        P("ctx", "head"),
    )
    return jax.shard_map(
        on_device, mesh=mesh, in_specs=in_specs, out_specs=out_specs, check_vma=False
    )
```

```python
from functools import reduce
import math

import jax
import jax.numpy as jnp
from jax import lax
from jax.sharding import PartitionSpec as P

WINDOW = 1024


norm_eps = 1e-06
rope_base = 10000.0


def passed_along(block, axis, distance):
    devices = range(lax.axis_size(axis))
    route = [(i - distance, i) for i in devices if i - distance in devices]
    return lax.ppermute(block, axis, route)


CORES = 2
Y_CHIPS = 4


def ring_pairs(rank_count, along_y):
    z_chips = rank_count // (CORES * Y_CHIPS)
    forward = []
    for z in range(z_chips):
        for y in range(Y_CHIPS):
            for core in range(CORES):
                source = (z * Y_CHIPS + y) * CORES + core
                if along_y:
                    target = (z * Y_CHIPS + (y + 1) % Y_CHIPS) * CORES + core
                else:
                    target = (((z + 1) % z_chips) * Y_CHIPS + y) * CORES + core
                forward.append((source, target))
    backward = [(target, source) for source, target in forward]
    return forward, backward


def ring_reduce_scatter(parts, axis, position, forward, backward):
    count = parts.shape[axis]
    half = parts.shape[-1] // 2

    def own(index, low):
        piece = lax.slice_in_dim(parts, low, low + half, axis=parts.ndim - 1)
        return lax.dynamic_index_in_dim(piece, index % count, axis, keepdims=False)

    up = own(position + count - 1, 0)
    down = own(position + 1, half)
    for step in range(count - 1):
        up = lax.ppermute(up.astype(jnp.bfloat16), "ctx", forward).astype(jnp.float32) + own(
            position + 2 * count - step - 2, 0
        )
        down = lax.ppermute(down.astype(jnp.bfloat16), "ctx", backward).astype(
            jnp.float32
        ) + own(position + step + 2, half)
    return jnp.concatenate([up, down], axis=-1)


def pair_rows(gathered, core, rank_count):
    z_chips = rank_count // (CORES * Y_CHIPS)
    count, width = gathered.shape
    grid = gathered.reshape(count, z_chips, Y_CHIPS, CORES, width // rank_count)
    return lax.dynamic_index_in_dim(grid, core, 3, keepdims=False).reshape(count, width // CORES)


def rounded_term(rows, columns):
    return (
        lax.dot_general(rows, columns, (((0,), (0,)), ((), ())), preferred_element_type=jnp.float32)
        .astype(jnp.bfloat16)
        .astype(jnp.float32)
    )


def torus_reduce_scatter(pair_sum, my_rank, rank_count):
    z_chips = rank_count // (CORES * Y_CHIPS)
    rows, columns = pair_sum.shape
    y_pos = (my_rank // CORES) % Y_CHIPS
    z_pos = my_rank // (CORES * Y_CHIPS)
    grid = pair_sum.reshape(z_chips, Y_CHIPS, rows // (z_chips * Y_CHIPS), columns)
    y_forward, y_backward = ring_pairs(rank_count, True)
    z_forward, z_backward = ring_pairs(rank_count, False)
    half = columns // 2
    first = grid[..., :half]
    second = grid[..., half:]
    first = ring_reduce_scatter(first, 1, y_pos, y_forward, y_backward)
    first = ring_reduce_scatter(first, 0, z_pos, z_forward, z_backward)
    second = ring_reduce_scatter(second, 0, z_pos, z_forward, z_backward)
    second = ring_reduce_scatter(second, 0, y_pos, y_forward, y_backward)
    return jnp.concatenate([first, second], axis=-1)


def rope_tables(positions, head_width):
    half_width = head_width // 2
    indices = jnp.arange(half_width, dtype=jnp.float32)
    frequency = jnp.power(rope_base, -2.0 * indices / head_width)
    angles = positions.astype(jnp.float32)[:, None] * frequency[None, :]
    return (jnp.cos(angles)[:, None, :], jnp.sin(angles)[:, None, :])


def rotate(vector, cosine_table, sine_table):
    half_width = vector.shape[-1] // 2
    lower_half = vector[..., :half_width]
    upper_half = vector[..., half_width:]
    return jnp.concatenate(
        [
            lower_half * cosine_table - upper_half * sine_table,
            upper_half * cosine_table + lower_half * sine_table,
        ],
        axis=-1,
    )


def unrotate(rotated, cosine_table, sine_table):
    half_width = rotated.shape[-1] // 2
    lower_half = rotated[..., :half_width]
    upper_half = rotated[..., half_width:]
    return jnp.concatenate(
        [
            lower_half * cosine_table + upper_half * sine_table,
            upper_half * cosine_table - lower_half * sine_table,
        ],
        axis=-1,
    )


def normalize(vector, gain_vector):
    inv_rms = lax.rsqrt(jnp.mean(vector * vector, axis=-1, keepdims=True) + norm_eps)
    return (vector * inv_rms * gain_vector, inv_rms)


def norm_back(vector, inv_rms, gain_vector, upstream):
    scaled = upstream * gain_vector
    return inv_rms * scaled - vector * (inv_rms * inv_rms * inv_rms) * jnp.mean(
        vector * scaled, axis=-1, keepdims=True
    )


def on_device(tokens, w_query, w_key, w_value, query_gain, key_gain, positions, out_grad):
    gathered = lax.all_gather(tokens, "head", axis=0, tiled=True)
    row_count = gathered.shape[0]
    head_width = query_gain.shape[0]
    head_count = w_query.shape[1] // head_width
    groups = w_key.shape[1] // head_width
    group_size = head_count // groups
    rank_count = lax.axis_size("ctx")
    my_rank = lax.axis_index("ctx")
    reach_blocks = min((WINDOW - 2) // row_count + 1, rank_count - 1)
    core = my_rank % CORES
    partner = [(rank, rank ^ 1) for rank in range(rank_count)]
    my_rows = pair_rows(gathered, core, rank_count)
    partner_rows = lax.ppermute(
        pair_rows(gathered, CORES - 1 - core, rank_count), "ctx", partner
    )
    query_scale = 1.0 / math.sqrt(head_width)
    query_raw = jnp.dot(gathered, w_query, preferred_element_type=jnp.float32).reshape(
        row_count, head_count, head_width
    )
    key_raw = jnp.dot(gathered, w_key, preferred_element_type=jnp.float32).reshape(
        row_count, groups, head_width
    )
    value_states = jnp.dot(gathered, w_value, preferred_element_type=jnp.float32).astype(
        jnp.bfloat16
    )
    cosine_table, sine_table = rope_tables(positions, head_width)
    query_normed, query_inv = normalize(query_raw, query_gain)
    key_normed, key_inv = normalize(key_raw, key_gain)
    query_states = (
        (rotate(query_normed, cosine_table, sine_table) * query_scale)
        .astype(jnp.bfloat16)
        .reshape(row_count, groups, group_size, head_width)
    )
    key_states = (
        rotate(key_normed, cosine_table, sine_table)
        .astype(jnp.bfloat16)
        .reshape(row_count, groups * head_width)
    )
    local_kv = jnp.stack([key_states, value_states])
    blocks = [local_kv]
    moving = local_kv
    for stride in range(reach_blocks):
        moving = passed_along(moving, "ctx", 1)
        blocks.append(moving)
    offsets = jnp.arange(row_count, dtype=jnp.int32)
    reach_limit = jnp.minimum(positions, WINDOW - 1)[:, None]
    visible_sets = []
    live_flags = []
    for stride in range(reach_blocks + 1):
        distance = stride * row_count + offsets[:, None] - offsets[None, :]
        visible = (distance >= 0) & (distance <= reach_limit) & (my_rank >= stride)
        visible_sets.append(visible)
        live_flags.append(jnp.any(visible))

    def block_keys(stride):
        return blocks[stride][0].reshape(row_count, groups, head_width)

    def block_values(stride):
        return blocks[stride][1].reshape(row_count, groups, head_width)

    def score_block(stride):
        return jnp.einsum(
            "qgue,kge->guqk", query_states, block_keys(stride), preferred_element_type=jnp.float32
        )

    scores = [score_block(stride) for stride in range(reach_blocks + 1)]
    row_peak = reduce(
        jnp.maximum,
        [
            jnp.max(
                jnp.where(visible_sets[stride], scores[stride], -jnp.inf), axis=-1, keepdims=True
            )
            for stride in range(reach_blocks + 1)
        ],
    )
    weights = [
        jnp.where(visible_sets[stride], jnp.exp(scores[stride] - row_peak), 0.0)
        for stride in range(reach_blocks + 1)
    ]
    row_total = reduce(
        jnp.add, [jnp.sum(weight_block, axis=-1, keepdims=True) for weight_block in weights]
    )
    probabilities = [weight_block / row_total for weight_block in weights]
    prob_bf16 = [prob_block.astype(jnp.bfloat16) for prob_block in probabilities]

    def mix_values(stride):
        return jnp.einsum(
            "guqk,kge->qgue",
            prob_bf16[stride],
            block_values(stride),
            preferred_element_type=jnp.float32,
        )

    mixed = reduce(jnp.add, [mix_values(stride) for stride in range(reach_blocks + 1)])
    attended = mixed.astype(jnp.bfloat16)
    grad_heads = out_grad.reshape(row_count, groups, group_size, head_width)
    row_delta = jnp.einsum(
        "qgue,qgue->guq", grad_heads, attended, preferred_element_type=jnp.float32
    )[..., None]

    def back_block(stride):
        key_block = block_keys(stride)
        dprobs = jnp.einsum(
            "qgue,kge->guqk", grad_heads, block_values(stride), preferred_element_type=jnp.float32
        )
        dscores = (probabilities[stride] * (dprobs - row_delta)).astype(jnp.bfloat16)
        query_grad = jnp.einsum(
            "guqk,kge->qgue", dscores, key_block, preferred_element_type=jnp.float32
        )
        key_grad = jnp.einsum(
            "guqk,qgue->kge", dscores, query_states, preferred_element_type=jnp.float32
        )
        value_grad = jnp.einsum(
            "guqk,qgue->kge", prob_bf16[stride], grad_heads, preferred_element_type=jnp.float32
        )
        return (
            query_grad,
            jnp.stack(
                [
                    key_grad.reshape(row_count, groups * head_width),
                    value_grad.reshape(row_count, groups * head_width),
                ]
            ),
        )

    back_terms = [back_block(stride) for stride in range(reach_blocks + 1)]
    query_grads = reduce(jnp.add, [term_pair[0] for term_pair in back_terms])
    key_grad_parts = [term_pair[1] for term_pair in back_terms]
    returned = key_grad_parts[reach_blocks]
    for stride in range(reach_blocks, 0, -1):
        returned = (
            passed_along(returned.astype(jnp.bfloat16), "ctx", -1).astype(returned.dtype)
            + key_grad_parts[stride - 1]
        )
    key_grads = returned[0].reshape(row_count, groups, head_width)
    value_grads = returned[1].astype(jnp.bfloat16)
    query_raw_grad = (
        norm_back(
            query_raw,
            query_inv,
            query_gain,
            unrotate(
                query_grads.reshape(row_count, head_count, head_width), cosine_table, sine_table
            )
            * query_scale,
        )
        .astype(jnp.bfloat16)
        .reshape(row_count, head_count * head_width)
    )
    key_raw_grad = (
        norm_back(key_raw, key_inv, key_gain, unrotate(key_grads, cosine_table, sine_table))
        .astype(jnp.bfloat16)
        .reshape(row_count, groups * head_width)
    )
    input_terms = (
        jnp.dot(query_raw_grad, w_query.T, preferred_element_type=jnp.float32)
        + jnp.dot(key_raw_grad, w_key.T, preferred_element_type=jnp.float32)
        + jnp.dot(value_grads, w_value.T, preferred_element_type=jnp.float32)
    )
    input_grad = lax.psum_scatter(
        input_terms.astype(jnp.bfloat16), "head", scatter_dimension=0, tiled=True
    )
    grad_columns = jnp.concatenate([query_raw_grad, key_raw_grad, value_grads], axis=1)
    partner_columns = lax.ppermute(grad_columns, "ctx", partner)
    pair_sum = rounded_term(my_rows, grad_columns) + rounded_term(partner_rows, partner_columns)
    summed = torus_reduce_scatter(pair_sum, my_rank, rank_count).astype(jnp.bfloat16)
    query_cols = head_count * head_width
    key_cols = groups * head_width
    return (
        attended.reshape(row_count, query_cols),
        input_grad,
        summed[:, :query_cols],
        summed[:, query_cols : query_cols + key_cols],
        summed[:, query_cols + key_cols :],
    )


def solution(mesh):
    in_specs = (
        P(("ctx", "head"), None),
        P(None, "head"),
        P(None, "head"),
        P(None, "head"),
        P(),
        P(),
        P("ctx"),
        P("ctx", "head"),
    )
    out_specs = (
        P("ctx", "head"),
        P(("ctx", "head"), None),
        P("ctx", "head"),
        P("ctx", "head"),
        P("ctx", "head"),
    )
    return jax.shard_map(
        on_device, mesh=mesh, in_specs=in_specs, out_specs=out_specs, check_vma=False
    )
```

```python
from functools import reduce
import math

import jax
import jax.numpy as jnp
from jax import lax
from jax.experimental import pallas as pl
from jax.experimental.pallas import tpu as pltpu
from jax.sharding import PartitionSpec as P

WINDOW = 1024


norm_eps = 1e-06
rope_base = 10000.0


def passed_along(block, axis, distance):
    devices = range(lax.axis_size(axis))
    route = [(i - distance, i) for i in devices if i - distance in devices]
    return lax.ppermute(block, axis, route)


CORES = 2
Y_CHIPS = 4


def ring_pairs(rank_count, along_y):
    z_chips = rank_count // (CORES * Y_CHIPS)
    forward = []
    for z in range(z_chips):
        for y in range(Y_CHIPS):
            for core in range(CORES):
                source = (z * Y_CHIPS + y) * CORES + core
                if along_y:
                    target = (z * Y_CHIPS + (y + 1) % Y_CHIPS) * CORES + core
                else:
                    target = (((z + 1) % z_chips) * Y_CHIPS + y) * CORES + core
                forward.append((source, target))
    backward = [(target, source) for source, target in forward]
    return forward, backward


def ring_reduce_scatter(parts, axis, position, forward, backward):
    count = parts.shape[axis]
    half = parts.shape[-1] // 2

    def own(index, low):
        piece = lax.slice_in_dim(parts, low, low + half, axis=parts.ndim - 1)
        return lax.dynamic_index_in_dim(piece, index % count, axis, keepdims=False)

    up = own(position + count - 1, 0)
    down = own(position + 1, half)
    for step in range(count - 1):
        up = lax.ppermute(up.astype(jnp.bfloat16), "ctx", forward).astype(jnp.float32) + own(
            position + 2 * count - step - 2, 0
        )
        down = lax.ppermute(down.astype(jnp.bfloat16), "ctx", backward).astype(
            jnp.float32
        ) + own(position + step + 2, half)
    return jnp.concatenate([up, down], axis=-1)


def pair_rows(gathered, core, rank_count):
    z_chips = rank_count // (CORES * Y_CHIPS)
    count, width = gathered.shape
    grid = gathered.reshape(count, z_chips, Y_CHIPS, CORES, width // rank_count)
    return lax.dynamic_index_in_dim(grid, core, 3, keepdims=False).reshape(count, width // CORES)


def rounded_term(rows, columns):
    return (
        lax.dot_general(rows, columns, (((0,), (0,)), ((), ())), preferred_element_type=jnp.float32)
        .astype(jnp.bfloat16)
        .astype(jnp.float32)
    )


def torus_reduce_scatter(pair_sum, my_rank, rank_count):
    z_chips = rank_count // (CORES * Y_CHIPS)
    rows, columns = pair_sum.shape
    y_pos = (my_rank // CORES) % Y_CHIPS
    z_pos = my_rank // (CORES * Y_CHIPS)
    grid = pair_sum.reshape(z_chips, Y_CHIPS, rows // (z_chips * Y_CHIPS), columns)
    y_forward, y_backward = ring_pairs(rank_count, True)
    z_forward, z_backward = ring_pairs(rank_count, False)
    half = columns // 2
    first = grid[..., :half]
    second = grid[..., half:]
    first = ring_reduce_scatter(first, 1, y_pos, y_forward, y_backward)
    first = ring_reduce_scatter(first, 0, z_pos, z_forward, z_backward)
    second = ring_reduce_scatter(second, 0, z_pos, z_forward, z_backward)
    second = ring_reduce_scatter(second, 0, y_pos, y_forward, y_backward)
    return jnp.concatenate([first, second], axis=-1)


def attention_body(q_ref, k_ref, v_ref, do_ref, lo_ref, att_ref, dq_ref, dk_ref, dv_ref):
    rows = q_ref.shape[0]
    keys, width = k_ref.shape
    k = k_ref[...]
    v = v_ref[...]
    key_index = lax.broadcasted_iota(jnp.int32, (rows, keys), 1)
    query_index = lax.broadcasted_iota(jnp.int32, (rows, keys), 0)
    visible = (key_index >= lo_ref[...]) & (key_index <= query_index + (keys - rows))
    dk = jnp.zeros((keys, width), jnp.float32)
    dv = jnp.zeros((keys, width), jnp.float32)
    for head in range(q_ref.shape[1] // width):
        cols = slice(head * width, (head + 1) * width)
        q = q_ref[:, cols]
        do = do_ref[:, cols]
        scores = lax.dot_general(q, k, (((1,), (1,)), ((), ())), preferred_element_type=jnp.float32)
        peak = jnp.max(jnp.where(visible, scores, -jnp.inf), axis=-1, keepdims=True)
        weights = jnp.where(visible, jnp.exp(scores - peak), 0.0)
        probs = weights / jnp.sum(weights, axis=-1, keepdims=True)
        probs_bf16 = probs.astype(jnp.bfloat16)
        attended = jnp.dot(probs_bf16, v, preferred_element_type=jnp.float32).astype(jnp.bfloat16)
        att_ref[:, cols] = attended
        delta = jnp.sum(
            do.astype(jnp.float32) * attended.astype(jnp.float32), axis=-1, keepdims=True
        )
        dprobs = lax.dot_general(do, v, (((1,), (1,)), ((), ())), preferred_element_type=jnp.float32)
        dscores = (probs * (dprobs - delta)).astype(jnp.bfloat16)
        dq_ref[:, cols] = jnp.dot(dscores, k, preferred_element_type=jnp.float32)
        dk = dk + lax.dot_general(
            dscores, q, (((0,), (0,)), ((), ())), preferred_element_type=jnp.float32
        )
        dv = dv + lax.dot_general(
            probs_bf16, do, (((0,), (0,)), ((), ())), preferred_element_type=jnp.float32
        )
    dk_ref[...] = dk
    dv_ref[...] = dv


def fused_attention(q2d, k_all, v_all, do2d, lower, groups):
    rows, query_cols = q2d.shape
    keys, kv_cols = k_all.shape
    width = kv_cols // groups
    per_group = query_cols // groups
    heads = query_cols // width
    flops = 2 * rows * keys * width * 6 * heads
    io_bytes = 2 * (3 * rows * query_cols + 2 * keys * kv_cols) + 4 * (rows * query_cols + 2 * keys * kv_cols)
    return pl.pallas_call(
        attention_body,
        grid=(groups,),
        in_specs=[
            pl.BlockSpec((rows, per_group), lambda g: (0, g)),
            pl.BlockSpec((keys, width), lambda g: (0, g)),
            pl.BlockSpec((keys, width), lambda g: (0, g)),
            pl.BlockSpec((rows, per_group), lambda g: (0, g)),
            pl.BlockSpec((rows, 1), lambda g: (0, 0)),
        ],
        out_specs=[
            pl.BlockSpec((rows, per_group), lambda g: (0, g)),
            pl.BlockSpec((rows, per_group), lambda g: (0, g)),
            pl.BlockSpec((keys, width), lambda g: (0, g)),
            pl.BlockSpec((keys, width), lambda g: (0, g)),
        ],
        out_shape=[
            jax.ShapeDtypeStruct((rows, query_cols), jnp.bfloat16),
            jax.ShapeDtypeStruct((rows, query_cols), jnp.float32),
            jax.ShapeDtypeStruct((keys, kv_cols), jnp.float32),
            jax.ShapeDtypeStruct((keys, kv_cols), jnp.float32),
        ],
        compiler_params=pltpu.CompilerParams(vmem_limit_bytes=56 * 1024 * 1024),
        cost_estimate=pl.CostEstimate(
            flops=flops, transcendentals=rows * keys * heads, bytes_accessed=io_bytes
        ),
    )(q2d, k_all, v_all, do2d, lower)


def rope_tables(positions, head_width):
    half_width = head_width // 2
    indices = jnp.arange(half_width, dtype=jnp.float32)
    frequency = jnp.power(rope_base, -2.0 * indices / head_width)
    angles = positions.astype(jnp.float32)[:, None] * frequency[None, :]
    return (jnp.cos(angles)[:, None, :], jnp.sin(angles)[:, None, :])


def rotate(vector, cosine_table, sine_table):
    half_width = vector.shape[-1] // 2
    lower_half = vector[..., :half_width]
    upper_half = vector[..., half_width:]
    return jnp.concatenate(
        [
            lower_half * cosine_table - upper_half * sine_table,
            upper_half * cosine_table + lower_half * sine_table,
        ],
        axis=-1,
    )


def unrotate(rotated, cosine_table, sine_table):
    half_width = rotated.shape[-1] // 2
    lower_half = rotated[..., :half_width]
    upper_half = rotated[..., half_width:]
    return jnp.concatenate(
        [
            lower_half * cosine_table + upper_half * sine_table,
            upper_half * cosine_table - lower_half * sine_table,
        ],
        axis=-1,
    )


def normalize(vector, gain_vector):
    inv_rms = lax.rsqrt(jnp.mean(vector * vector, axis=-1, keepdims=True) + norm_eps)
    return (vector * inv_rms * gain_vector, inv_rms)


def norm_back(vector, inv_rms, gain_vector, upstream):
    scaled = upstream * gain_vector
    return inv_rms * scaled - vector * (inv_rms * inv_rms * inv_rms) * jnp.mean(
        vector * scaled, axis=-1, keepdims=True
    )


def on_device(tokens, w_query, w_key, w_value, query_gain, key_gain, positions, out_grad):
    gathered = lax.all_gather(tokens, "head", axis=0, tiled=True)
    row_count = gathered.shape[0]
    head_width = query_gain.shape[0]
    head_count = w_query.shape[1] // head_width
    groups = w_key.shape[1] // head_width
    group_size = head_count // groups
    rank_count = lax.axis_size("ctx")
    my_rank = lax.axis_index("ctx")
    reach_blocks = min((WINDOW - 2) // row_count + 1, rank_count - 1)
    core = my_rank % CORES
    partner = [(rank, rank ^ 1) for rank in range(rank_count)]
    my_rows = pair_rows(gathered, core, rank_count)
    partner_rows = lax.ppermute(
        pair_rows(gathered, CORES - 1 - core, rank_count), "ctx", partner
    )
    query_scale = 1.0 / math.sqrt(head_width)
    query_raw = jnp.dot(gathered, w_query, preferred_element_type=jnp.float32).reshape(
        row_count, head_count, head_width
    )
    key_raw = jnp.dot(gathered, w_key, preferred_element_type=jnp.float32).reshape(
        row_count, groups, head_width
    )
    value_states = jnp.dot(gathered, w_value, preferred_element_type=jnp.float32).astype(
        jnp.bfloat16
    )
    cosine_table, sine_table = rope_tables(positions, head_width)
    query_normed, query_inv = normalize(query_raw, query_gain)
    key_normed, key_inv = normalize(key_raw, key_gain)
    query_states = (
        (rotate(query_normed, cosine_table, sine_table) * query_scale)
        .astype(jnp.bfloat16)
        .reshape(row_count, groups, group_size, head_width)
    )
    key_states = (
        rotate(key_normed, cosine_table, sine_table)
        .astype(jnp.bfloat16)
        .reshape(row_count, groups * head_width)
    )
    local_kv = jnp.stack([key_states, value_states])
    blocks = [local_kv]
    moving = local_kv
    for stride in range(reach_blocks):
        moving = passed_along(moving, "ctx", 1)
        blocks.append(moving)
    offsets = jnp.arange(row_count, dtype=jnp.int32)
    key_count = (reach_blocks + 1) * row_count
    lower = jnp.maximum(
        (reach_blocks - my_rank) * row_count,
        reach_blocks * row_count + offsets - jnp.minimum(positions, WINDOW - 1),
    )[:, None]
    ordered = blocks[::-1]
    all_keys = jnp.concatenate([block[0] for block in ordered], axis=0)
    all_values = jnp.concatenate([block[1] for block in ordered], axis=0)
    attended, query_grads, key_grad_all, value_grad_all = fused_attention(
        query_states.reshape(row_count, head_count * head_width),
        all_keys,
        all_values,
        out_grad,
        lower,
        groups,
    )

    def grad_rows(stride):
        start = key_count - (stride + 1) * row_count
        return jnp.stack(
            [
                key_grad_all[start : start + row_count],
                value_grad_all[start : start + row_count],
            ]
        )

    key_grad_parts = [grad_rows(stride) for stride in range(reach_blocks + 1)]
    returned = key_grad_parts[reach_blocks]
    for stride in range(reach_blocks, 0, -1):
        returned = (
            passed_along(returned.astype(jnp.bfloat16), "ctx", -1).astype(returned.dtype)
            + key_grad_parts[stride - 1]
        )
    key_grads = returned[0].reshape(row_count, groups, head_width)
    value_grads = returned[1].astype(jnp.bfloat16)
    query_raw_grad = (
        norm_back(
            query_raw,
            query_inv,
            query_gain,
            unrotate(
                query_grads.reshape(row_count, head_count, head_width), cosine_table, sine_table
            )
            * query_scale,
        )
        .astype(jnp.bfloat16)
        .reshape(row_count, head_count * head_width)
    )
    key_raw_grad = (
        norm_back(key_raw, key_inv, key_gain, unrotate(key_grads, cosine_table, sine_table))
        .astype(jnp.bfloat16)
        .reshape(row_count, groups * head_width)
    )
    input_terms = (
        jnp.dot(query_raw_grad, w_query.T, preferred_element_type=jnp.float32)
        + jnp.dot(key_raw_grad, w_key.T, preferred_element_type=jnp.float32)
        + jnp.dot(value_grads, w_value.T, preferred_element_type=jnp.float32)
    )
    input_grad = lax.psum_scatter(
        input_terms.astype(jnp.bfloat16), "head", scatter_dimension=0, tiled=True
    )
    grad_columns = jnp.concatenate([query_raw_grad, key_raw_grad, value_grads], axis=1)
    partner_columns = lax.ppermute(grad_columns, "ctx", partner)
    pair_sum = rounded_term(my_rows, grad_columns) + rounded_term(partner_rows, partner_columns)
    summed = torus_reduce_scatter(pair_sum, my_rank, rank_count).astype(jnp.bfloat16)
    query_cols = head_count * head_width
    key_cols = groups * head_width
    return (
        attended.reshape(row_count, query_cols),
        input_grad,
        summed[:, :query_cols],
        summed[:, query_cols : query_cols + key_cols],
        summed[:, query_cols + key_cols :],
    )


def solution(mesh):
    in_specs = (
        P(("ctx", "head"), None),
        P(None, "head"),
        P(None, "head"),
        P(None, "head"),
        P(),
        P(),
        P("ctx"),
        P("ctx", "head"),
    )
    out_specs = (
        P("ctx", "head"),
        P(("ctx", "head"), None),
        P("ctx", "head"),
        P("ctx", "head"),
        P("ctx", "head"),
    )
    return jax.shard_map(
        on_device, mesh=mesh, in_specs=in_specs, out_specs=out_specs, check_vma=False
    )
```

```python
from functools import reduce
import math

import jax
import jax.numpy as jnp
from jax import lax
from jax.experimental import pallas as pl
from jax.experimental.pallas import tpu as pltpu
from jax.sharding import PartitionSpec as P

WINDOW = 1024


norm_eps = 1e-06
rope_base = 10000.0


def passed_along(block, axis, distance):
    devices = range(lax.axis_size(axis))
    route = [(i - distance, i) for i in devices if i - distance in devices]
    return lax.ppermute(block, axis, route)


CORES = 2
Y_CHIPS = 4


def ring_pairs(rank_count, along_y):
    z_chips = rank_count // (CORES * Y_CHIPS)
    forward = []
    for z in range(z_chips):
        for y in range(Y_CHIPS):
            for core in range(CORES):
                source = (z * Y_CHIPS + y) * CORES + core
                if along_y:
                    target = (z * Y_CHIPS + (y + 1) % Y_CHIPS) * CORES + core
                else:
                    target = (((z + 1) % z_chips) * Y_CHIPS + y) * CORES + core
                forward.append((source, target))
    backward = [(target, source) for source, target in forward]
    return forward, backward


def ring_reduce_scatter(parts, axis, position, forward, backward):
    count = parts.shape[axis]
    half = parts.shape[-1] // 2

    def own(index, low):
        piece = lax.slice_in_dim(parts, low, low + half, axis=parts.ndim - 1)
        return lax.dynamic_index_in_dim(piece, index % count, axis, keepdims=False)

    def send(value, pairs):
        return lax.ppermute(value.astype(jnp.bfloat16), "ctx", pairs).astype(jnp.float32)

    if count == 4:
        quarter = half // 2
        up_first = send(
            jnp.concatenate([own(position + 2, 0), own(position + 1, half)], axis=-1), forward
        )
        down_first = send(
            jnp.concatenate([own(position + 2, half), own(position + 3, 0)], axis=-1), backward
        )
        up_second = send(up_first[..., :half] + own(position + 1, 0), forward)
        down_second = send(down_first[..., :half] + own(position + 3, half), backward)
        low_half = own(position, 0) + up_second + down_first[..., half:]
        high_half = own(position, half) + down_second + up_first[..., half:]
        return jnp.concatenate([low_half, high_half], axis=-1)

    up = own(position + count - 1, 0)
    down = own(position + 1, half)
    for step in range(count - 1):
        up = send(up, forward) + own(position + 2 * count - step - 2, 0)
        down = send(down, backward) + own(position + step + 2, half)
    return jnp.concatenate([up, down], axis=-1)


def pair_rows(gathered, core, rank_count):
    z_chips = rank_count // (CORES * Y_CHIPS)
    count, width = gathered.shape
    grid = gathered.reshape(count, z_chips, Y_CHIPS, CORES, width // rank_count)
    return lax.dynamic_index_in_dim(grid, core, 3, keepdims=False).reshape(count, width // CORES)


def rounded_term(rows, columns):
    return (
        lax.dot_general(rows, columns, (((0,), (0,)), ((), ())), preferred_element_type=jnp.float32)
        .astype(jnp.bfloat16)
        .astype(jnp.float32)
    )


def torus_reduce_scatter(pair_sum, my_rank, rank_count):
    z_chips = rank_count // (CORES * Y_CHIPS)
    rows, columns = pair_sum.shape
    y_pos = (my_rank // CORES) % Y_CHIPS
    z_pos = my_rank // (CORES * Y_CHIPS)
    grid = pair_sum.reshape(z_chips, Y_CHIPS, rows // (z_chips * Y_CHIPS), columns)
    y_forward, y_backward = ring_pairs(rank_count, True)
    z_forward, z_backward = ring_pairs(rank_count, False)
    half = columns // 2
    first = grid[..., :half]
    second = grid[..., half:]
    first = ring_reduce_scatter(first, 1, y_pos, y_forward, y_backward)
    first = ring_reduce_scatter(first, 0, z_pos, z_forward, z_backward)
    second = ring_reduce_scatter(second, 0, z_pos, z_forward, z_backward)
    second = ring_reduce_scatter(second, 0, y_pos, y_forward, y_backward)
    return jnp.concatenate([first, second], axis=-1)


def attention_body(q_ref, k_ref, v_ref, do_ref, lo_ref, att_ref, dq_ref, dk_ref, dv_ref):
    rows = q_ref.shape[0]
    keys, width = k_ref.shape
    k = k_ref[...]
    v = v_ref[...]
    key_index = lax.broadcasted_iota(jnp.int32, (rows, keys), 1)
    query_index = lax.broadcasted_iota(jnp.int32, (rows, keys), 0)
    visible = (key_index >= lo_ref[...]) & (key_index <= query_index + (keys - rows))
    dk = jnp.zeros((keys, width), jnp.float32)
    dv = jnp.zeros((keys, width), jnp.float32)
    for head in range(q_ref.shape[1] // width):
        cols = slice(head * width, (head + 1) * width)
        q = q_ref[:, cols]
        do = do_ref[:, cols]
        scores = lax.dot_general(q, k, (((1,), (1,)), ((), ())), preferred_element_type=jnp.float32)
        peak = jnp.max(jnp.where(visible, scores, -jnp.inf), axis=-1, keepdims=True)
        weights = jnp.where(visible, jnp.exp(scores - peak), 0.0)
        probs = weights / jnp.sum(weights, axis=-1, keepdims=True)
        probs_bf16 = probs.astype(jnp.bfloat16)
        attended = jnp.dot(probs_bf16, v, preferred_element_type=jnp.float32).astype(jnp.bfloat16)
        att_ref[:, cols] = attended
        delta = jnp.sum(
            do.astype(jnp.float32) * attended.astype(jnp.float32), axis=-1, keepdims=True
        )
        dprobs = lax.dot_general(do, v, (((1,), (1,)), ((), ())), preferred_element_type=jnp.float32)
        dscores = (probs * (dprobs - delta)).astype(jnp.bfloat16)
        dq_ref[:, cols] = jnp.dot(dscores, k, preferred_element_type=jnp.float32)
        dk = dk + lax.dot_general(
            dscores, q, (((0,), (0,)), ((), ())), preferred_element_type=jnp.float32
        )
        dv = dv + lax.dot_general(
            probs_bf16, do, (((0,), (0,)), ((), ())), preferred_element_type=jnp.float32
        )
    dk_ref[...] = dk
    dv_ref[...] = dv


def fused_attention(q2d, k_all, v_all, do2d, lower, groups):
    rows, query_cols = q2d.shape
    keys, kv_cols = k_all.shape
    width = kv_cols // groups
    per_group = query_cols // groups
    heads = query_cols // width
    flops = 2 * rows * keys * width * 6 * heads
    io_bytes = 2 * (3 * rows * query_cols + 2 * keys * kv_cols) + 4 * (rows * query_cols + 2 * keys * kv_cols)
    return pl.pallas_call(
        attention_body,
        grid=(groups,),
        in_specs=[
            pl.BlockSpec((rows, per_group), lambda g: (0, g)),
            pl.BlockSpec((keys, width), lambda g: (0, g)),
            pl.BlockSpec((keys, width), lambda g: (0, g)),
            pl.BlockSpec((rows, per_group), lambda g: (0, g)),
            pl.BlockSpec((rows, 1), lambda g: (0, 0)),
        ],
        out_specs=[
            pl.BlockSpec((rows, per_group), lambda g: (0, g)),
            pl.BlockSpec((rows, per_group), lambda g: (0, g)),
            pl.BlockSpec((keys, width), lambda g: (0, g)),
            pl.BlockSpec((keys, width), lambda g: (0, g)),
        ],
        out_shape=[
            jax.ShapeDtypeStruct((rows, query_cols), jnp.bfloat16),
            jax.ShapeDtypeStruct((rows, query_cols), jnp.float32),
            jax.ShapeDtypeStruct((keys, kv_cols), jnp.float32),
            jax.ShapeDtypeStruct((keys, kv_cols), jnp.float32),
        ],
        compiler_params=pltpu.CompilerParams(vmem_limit_bytes=56 * 1024 * 1024),
        cost_estimate=pl.CostEstimate(
            flops=flops, transcendentals=rows * keys * heads, bytes_accessed=io_bytes
        ),
    )(q2d, k_all, v_all, do2d, lower)


def rope_tables(positions, head_width):
    half_width = head_width // 2
    indices = jnp.arange(half_width, dtype=jnp.float32)
    frequency = jnp.power(rope_base, -2.0 * indices / head_width)
    angles = positions.astype(jnp.float32)[:, None] * frequency[None, :]
    return (jnp.cos(angles)[:, None, :], jnp.sin(angles)[:, None, :])


def rotate(vector, cosine_table, sine_table):
    half_width = vector.shape[-1] // 2
    lower_half = vector[..., :half_width]
    upper_half = vector[..., half_width:]
    return jnp.concatenate(
        [
            lower_half * cosine_table - upper_half * sine_table,
            upper_half * cosine_table + lower_half * sine_table,
        ],
        axis=-1,
    )


def unrotate(rotated, cosine_table, sine_table):
    half_width = rotated.shape[-1] // 2
    lower_half = rotated[..., :half_width]
    upper_half = rotated[..., half_width:]
    return jnp.concatenate(
        [
            lower_half * cosine_table + upper_half * sine_table,
            upper_half * cosine_table - lower_half * sine_table,
        ],
        axis=-1,
    )


def normalize(vector, gain_vector):
    inv_rms = lax.rsqrt(jnp.mean(vector * vector, axis=-1, keepdims=True) + norm_eps)
    return (vector * inv_rms * gain_vector, inv_rms)


def norm_back(vector, inv_rms, gain_vector, upstream):
    scaled = upstream * gain_vector
    return inv_rms * scaled - vector * (inv_rms * inv_rms * inv_rms) * jnp.mean(
        vector * scaled, axis=-1, keepdims=True
    )


def on_device(tokens, w_query, w_key, w_value, query_gain, key_gain, positions, out_grad):
    gathered = lax.all_gather(tokens, "head", axis=0, tiled=True)
    row_count = gathered.shape[0]
    head_width = query_gain.shape[0]
    head_count = w_query.shape[1] // head_width
    groups = w_key.shape[1] // head_width
    group_size = head_count // groups
    rank_count = lax.axis_size("ctx")
    my_rank = lax.axis_index("ctx")
    reach_blocks = min((WINDOW - 2) // row_count + 1, rank_count - 1)
    core = my_rank % CORES
    partner = [(rank, rank ^ 1) for rank in range(rank_count)]
    my_rows = pair_rows(gathered, core, rank_count)
    partner_rows = lax.ppermute(
        pair_rows(gathered, CORES - 1 - core, rank_count), "ctx", partner
    )
    query_scale = 1.0 / math.sqrt(head_width)
    query_raw = jnp.dot(gathered, w_query, preferred_element_type=jnp.float32).reshape(
        row_count, head_count, head_width
    )
    key_raw = jnp.dot(gathered, w_key, preferred_element_type=jnp.float32).reshape(
        row_count, groups, head_width
    )
    value_states = jnp.dot(gathered, w_value, preferred_element_type=jnp.float32).astype(
        jnp.bfloat16
    )
    cosine_table, sine_table = rope_tables(positions, head_width)
    query_normed, query_inv = normalize(query_raw, query_gain)
    key_normed, key_inv = normalize(key_raw, key_gain)
    query_states = (
        (rotate(query_normed, cosine_table, sine_table) * query_scale)
        .astype(jnp.bfloat16)
        .reshape(row_count, groups, group_size, head_width)
    )
    key_states = (
        rotate(key_normed, cosine_table, sine_table)
        .astype(jnp.bfloat16)
        .reshape(row_count, groups * head_width)
    )
    local_kv = jnp.stack([key_states, value_states])
    blocks = [local_kv]
    moving = local_kv
    for stride in range(reach_blocks):
        moving = passed_along(moving, "ctx", 1)
        blocks.append(moving)
    offsets = jnp.arange(row_count, dtype=jnp.int32)
    key_count = (reach_blocks + 1) * row_count
    lower = jnp.maximum(
        (reach_blocks - my_rank) * row_count,
        reach_blocks * row_count + offsets - jnp.minimum(positions, WINDOW - 1),
    )[:, None]
    ordered = blocks[::-1]
    all_keys = jnp.concatenate([block[0] for block in ordered], axis=0)
    all_values = jnp.concatenate([block[1] for block in ordered], axis=0)
    attended, query_grads, key_grad_all, value_grad_all = fused_attention(
        query_states.reshape(row_count, head_count * head_width),
        all_keys,
        all_values,
        out_grad,
        lower,
        groups,
    )

    def grad_rows(stride):
        start = key_count - (stride + 1) * row_count
        return jnp.stack(
            [
                key_grad_all[start : start + row_count],
                value_grad_all[start : start + row_count],
            ]
        )

    key_grad_parts = [grad_rows(stride) for stride in range(reach_blocks + 1)]
    returned = key_grad_parts[reach_blocks]
    for stride in range(reach_blocks, 0, -1):
        returned = (
            passed_along(returned.astype(jnp.bfloat16), "ctx", -1).astype(returned.dtype)
            + key_grad_parts[stride - 1]
        )
    key_grads = returned[0].reshape(row_count, groups, head_width)
    value_grads = returned[1].astype(jnp.bfloat16)
    query_raw_grad = (
        norm_back(
            query_raw,
            query_inv,
            query_gain,
            unrotate(
                query_grads.reshape(row_count, head_count, head_width), cosine_table, sine_table
            )
            * query_scale,
        )
        .astype(jnp.bfloat16)
        .reshape(row_count, head_count * head_width)
    )
    key_raw_grad = (
        norm_back(key_raw, key_inv, key_gain, unrotate(key_grads, cosine_table, sine_table))
        .astype(jnp.bfloat16)
        .reshape(row_count, groups * head_width)
    )
    input_terms = (
        jnp.dot(query_raw_grad, w_query.T, preferred_element_type=jnp.float32)
        + jnp.dot(key_raw_grad, w_key.T, preferred_element_type=jnp.float32)
        + jnp.dot(value_grads, w_value.T, preferred_element_type=jnp.float32)
    )
    input_grad = lax.psum_scatter(
        input_terms.astype(jnp.bfloat16), "head", scatter_dimension=0, tiled=True
    )
    grad_columns = jnp.concatenate([query_raw_grad, key_raw_grad, value_grads], axis=1)
    partner_columns = lax.ppermute(grad_columns, "ctx", partner)
    pair_sum = rounded_term(my_rows, grad_columns) + rounded_term(partner_rows, partner_columns)
    summed = torus_reduce_scatter(pair_sum, my_rank, rank_count).astype(jnp.bfloat16)
    query_cols = head_count * head_width
    key_cols = groups * head_width
    return (
        attended.reshape(row_count, query_cols),
        input_grad,
        summed[:, :query_cols],
        summed[:, query_cols : query_cols + key_cols],
        summed[:, query_cols + key_cols :],
    )


def solution(mesh):
    in_specs = (
        P(("ctx", "head"), None),
        P(None, "head"),
        P(None, "head"),
        P(None, "head"),
        P(),
        P(),
        P("ctx"),
        P("ctx", "head"),
    )
    out_specs = (
        P("ctx", "head"),
        P(("ctx", "head"), None),
        P("ctx", "head"),
        P("ctx", "head"),
        P("ctx", "head"),
    )
    return jax.shard_map(
        on_device, mesh=mesh, in_specs=in_specs, out_specs=out_specs, check_vma=False
    )
```

```python
from functools import reduce
import math

import jax
import jax.numpy as jnp
from jax import lax
from jax.experimental import pallas as pl
from jax.experimental.pallas import tpu as pltpu
from jax.sharding import PartitionSpec as P

WINDOW = 1024


norm_eps = 1e-06
rope_base = 10000.0


def passed_along(block, axis, distance):
    devices = range(lax.axis_size(axis))
    route = [(i - distance, i) for i in devices if i - distance in devices]
    return lax.ppermute(block, axis, route)


CORES = 2
Y_CHIPS = 4


def ring_pairs(rank_count, along_y):
    z_chips = rank_count // (CORES * Y_CHIPS)
    forward = []
    for z in range(z_chips):
        for y in range(Y_CHIPS):
            for core in range(CORES):
                source = (z * Y_CHIPS + y) * CORES + core
                if along_y:
                    target = (z * Y_CHIPS + (y + 1) % Y_CHIPS) * CORES + core
                else:
                    target = (((z + 1) % z_chips) * Y_CHIPS + y) * CORES + core
                forward.append((source, target))
    backward = [(target, source) for source, target in forward]
    return forward, backward


def ring_reduce_scatter(parts, axis, position, forward, backward):
    count = parts.shape[axis]
    half = parts.shape[-1] // 2

    def own(index, low):
        piece = lax.slice_in_dim(parts, low, low + half, axis=parts.ndim - 1)
        return lax.dynamic_index_in_dim(piece, index % count, axis, keepdims=False)

    up = own(position + count - 1, 0)
    down = own(position + 1, half)
    for step in range(count - 1):
        up = lax.ppermute(up.astype(jnp.bfloat16), "ctx", forward).astype(jnp.float32) + own(
            position + 2 * count - step - 2, 0
        )
        down = lax.ppermute(down.astype(jnp.bfloat16), "ctx", backward).astype(
            jnp.float32
        ) + own(position + step + 2, half)
    return jnp.concatenate([up, down], axis=-1)


def pair_rows(gathered, core, rank_count):
    z_chips = rank_count // (CORES * Y_CHIPS)
    count, width = gathered.shape
    grid = gathered.reshape(count, z_chips, Y_CHIPS, CORES, width // rank_count)
    return lax.dynamic_index_in_dim(grid, core, 3, keepdims=False).reshape(count, width // CORES)


def rounded_term(rows, columns):
    return (
        lax.dot_general(rows, columns, (((0,), (0,)), ((), ())), preferred_element_type=jnp.float32)
        .astype(jnp.bfloat16)
        .astype(jnp.float32)
    )


def torus_reduce_scatter(pair_sum, my_rank, rank_count):
    z_chips = rank_count // (CORES * Y_CHIPS)
    rows, columns = pair_sum.shape
    y_pos = (my_rank // CORES) % Y_CHIPS
    z_pos = my_rank // (CORES * Y_CHIPS)
    grid = pair_sum.reshape(z_chips, Y_CHIPS, rows // (z_chips * Y_CHIPS), columns)
    y_forward, y_backward = ring_pairs(rank_count, True)
    z_forward, z_backward = ring_pairs(rank_count, False)
    half = columns // 2
    first = grid[..., :half]
    second = grid[..., half:]
    first = ring_reduce_scatter(first, 1, y_pos, y_forward, y_backward)
    first = ring_reduce_scatter(first, 0, z_pos, z_forward, z_backward)
    second = ring_reduce_scatter(second, 0, z_pos, z_forward, z_backward)
    second = ring_reduce_scatter(second, 0, y_pos, y_forward, y_backward)
    return jnp.concatenate([first, second], axis=-1)


def attention_body(q_ref, k_ref, v_ref, do_ref, lo_ref, att_ref, dq_ref, dk_ref, dv_ref):
    rows = q_ref.shape[0]
    keys, width = k_ref.shape
    k = k_ref[...]
    v = v_ref[...]
    key_index = lax.broadcasted_iota(jnp.int32, (rows, keys), 1)
    query_index = lax.broadcasted_iota(jnp.int32, (rows, keys), 0)
    visible = (key_index >= lo_ref[...]) & (key_index <= query_index + (keys - rows))
    dk = jnp.zeros((keys, width), jnp.float32)
    dv = jnp.zeros((keys, width), jnp.float32)
    for head in range(q_ref.shape[1] // width):
        cols = slice(head * width, (head + 1) * width)
        q = q_ref[:, cols]
        do = do_ref[:, cols]
        scores = lax.dot_general(q, k, (((1,), (1,)), ((), ())), preferred_element_type=jnp.float32)
        peak = jnp.max(jnp.where(visible, scores, -jnp.inf), axis=-1, keepdims=True)
        weights = jnp.where(visible, jnp.exp(scores - peak), 0.0)
        probs = weights / jnp.sum(weights, axis=-1, keepdims=True)
        probs_bf16 = probs.astype(jnp.bfloat16)
        attended = jnp.dot(probs_bf16, v, preferred_element_type=jnp.float32).astype(jnp.bfloat16)
        att_ref[:, cols] = attended
        delta = jnp.sum(
            do.astype(jnp.float32) * attended.astype(jnp.float32), axis=-1, keepdims=True
        )
        dprobs = lax.dot_general(do, v, (((1,), (1,)), ((), ())), preferred_element_type=jnp.float32)
        dscores = (probs * (dprobs - delta)).astype(jnp.bfloat16)
        dq_ref[:, cols] = jnp.dot(dscores, k, preferred_element_type=jnp.float32)
        dk = dk + lax.dot_general(
            dscores, q, (((0,), (0,)), ((), ())), preferred_element_type=jnp.float32
        )
        dv = dv + lax.dot_general(
            probs_bf16, do, (((0,), (0,)), ((), ())), preferred_element_type=jnp.float32
        )
    dk_ref[...] = dk
    dv_ref[...] = dv


def fused_attention(q2d, k_all, v_all, do2d, lower, groups):
    rows, query_cols = q2d.shape
    keys, kv_cols = k_all.shape
    width = kv_cols // groups
    per_group = query_cols // groups
    heads = query_cols // width
    flops = 2 * rows * keys * width * 6 * heads
    io_bytes = 2 * (3 * rows * query_cols + 2 * keys * kv_cols) + 4 * (rows * query_cols + 2 * keys * kv_cols)
    return pl.pallas_call(
        attention_body,
        grid=(groups,),
        in_specs=[
            pl.BlockSpec((rows, per_group), lambda g: (0, g)),
            pl.BlockSpec((keys, width), lambda g: (0, g)),
            pl.BlockSpec((keys, width), lambda g: (0, g)),
            pl.BlockSpec((rows, per_group), lambda g: (0, g)),
            pl.BlockSpec((rows, 1), lambda g: (0, 0)),
        ],
        out_specs=[
            pl.BlockSpec((rows, per_group), lambda g: (0, g)),
            pl.BlockSpec((rows, per_group), lambda g: (0, g)),
            pl.BlockSpec((keys, width), lambda g: (0, g)),
            pl.BlockSpec((keys, width), lambda g: (0, g)),
        ],
        out_shape=[
            jax.ShapeDtypeStruct((rows, query_cols), jnp.bfloat16),
            jax.ShapeDtypeStruct((rows, query_cols), jnp.float32),
            jax.ShapeDtypeStruct((keys, kv_cols), jnp.float32),
            jax.ShapeDtypeStruct((keys, kv_cols), jnp.float32),
        ],
        compiler_params=pltpu.CompilerParams(vmem_limit_bytes=56 * 1024 * 1024),
        cost_estimate=pl.CostEstimate(
            flops=flops, transcendentals=rows * keys * heads, bytes_accessed=io_bytes
        ),
    )(q2d, k_all, v_all, do2d, lower)


def rope_tables(positions, head_width):
    half_width = head_width // 2
    indices = jnp.arange(half_width, dtype=jnp.float32)
    frequency = jnp.power(rope_base, -2.0 * indices / head_width)
    angles = positions.astype(jnp.float32)[:, None] * frequency[None, :]
    return (jnp.cos(angles)[:, None, :], jnp.sin(angles)[:, None, :])


def rotate(vector, cosine_table, sine_table):
    half_width = vector.shape[-1] // 2
    lower_half = vector[..., :half_width]
    upper_half = vector[..., half_width:]
    return jnp.concatenate(
        [
            lower_half * cosine_table - upper_half * sine_table,
            upper_half * cosine_table + lower_half * sine_table,
        ],
        axis=-1,
    )


def unrotate(rotated, cosine_table, sine_table):
    half_width = rotated.shape[-1] // 2
    lower_half = rotated[..., :half_width]
    upper_half = rotated[..., half_width:]
    return jnp.concatenate(
        [
            lower_half * cosine_table + upper_half * sine_table,
            upper_half * cosine_table - lower_half * sine_table,
        ],
        axis=-1,
    )


def normalize(vector, gain_vector):
    inv_rms = lax.rsqrt(jnp.mean(vector * vector, axis=-1, keepdims=True) + norm_eps)
    return (vector * inv_rms * gain_vector, inv_rms)


def norm_back(vector, inv_rms, gain_vector, upstream):
    scaled = upstream * gain_vector
    return inv_rms * scaled - vector * (inv_rms * inv_rms * inv_rms) * jnp.mean(
        vector * scaled, axis=-1, keepdims=True
    )


def on_device(tokens, w_query, w_key, w_value, query_gain, key_gain, positions, out_grad):
    gathered = lax.all_gather(tokens, "head", axis=0, tiled=True)
    row_count = gathered.shape[0]
    head_width = query_gain.shape[0]
    head_count = w_query.shape[1] // head_width
    groups = w_key.shape[1] // head_width
    group_size = head_count // groups
    rank_count = lax.axis_size("ctx")
    my_rank = lax.axis_index("ctx")
    reach_blocks = min((WINDOW - 2) // row_count + 1, rank_count - 1)
    core = my_rank % CORES
    partner = [(rank, rank ^ 1) for rank in range(rank_count)]
    my_rows = pair_rows(gathered, core, rank_count)
    partner_rows = lax.ppermute(
        pair_rows(gathered, CORES - 1 - core, rank_count), "ctx", partner
    )
    query_scale = 1.0 / math.sqrt(head_width)
    query_raw = jnp.dot(gathered, w_query, preferred_element_type=jnp.float32).reshape(
        row_count, head_count, head_width
    )
    key_raw = jnp.dot(gathered, w_key, preferred_element_type=jnp.float32).reshape(
        row_count, groups, head_width
    )
    value_states = jnp.dot(gathered, w_value, preferred_element_type=jnp.float32).astype(
        jnp.bfloat16
    )
    cosine_table, sine_table = rope_tables(positions, head_width)
    query_normed, query_inv = normalize(query_raw, query_gain)
    key_normed, key_inv = normalize(key_raw, key_gain)
    query_states = (
        (rotate(query_normed, cosine_table, sine_table) * query_scale)
        .astype(jnp.bfloat16)
        .reshape(row_count, groups, group_size, head_width)
    )
    key_states = (
        rotate(key_normed, cosine_table, sine_table)
        .astype(jnp.bfloat16)
        .reshape(row_count, groups * head_width)
    )
    local_kv = jnp.stack([key_states, value_states])
    blocks = [local_kv]
    moving = local_kv
    for stride in range(reach_blocks):
        moving = passed_along(moving, "ctx", 1)
        blocks.append(moving)
    offsets = jnp.arange(row_count, dtype=jnp.int32)
    key_count = (reach_blocks + 1) * row_count
    lower = jnp.maximum(
        (reach_blocks - my_rank) * row_count,
        reach_blocks * row_count + offsets - jnp.minimum(positions, WINDOW - 1),
    )[:, None]
    ordered = blocks[::-1]
    all_keys = jnp.concatenate([block[0] for block in ordered], axis=0)
    all_values = jnp.concatenate([block[1] for block in ordered], axis=0)
    attended, query_grads, key_grad_all, value_grad_all = fused_attention(
        query_states.reshape(row_count, head_count * head_width),
        all_keys,
        all_values,
        out_grad,
        lower,
        groups,
    )

    def grad_rows(stride):
        start = key_count - (stride + 1) * row_count
        return jnp.stack(
            [
                key_grad_all[start : start + row_count],
                value_grad_all[start : start + row_count],
            ]
        )

    key_grad_parts = [grad_rows(stride) for stride in range(reach_blocks + 1)]
    returned = key_grad_parts[reach_blocks]
    for stride in range(reach_blocks, 0, -1):
        returned = (
            passed_along(returned.astype(jnp.bfloat16), "ctx", -1).astype(returned.dtype)
            + key_grad_parts[stride - 1]
        )
    key_grads = returned[0].reshape(row_count, groups, head_width)
    value_grads = returned[1].astype(jnp.bfloat16)
    query_raw_grad = (
        norm_back(
            query_raw,
            query_inv,
            query_gain,
            unrotate(
                query_grads.reshape(row_count, head_count, head_width), cosine_table, sine_table
            )
            * query_scale,
        )
        .astype(jnp.bfloat16)
        .reshape(row_count, head_count * head_width)
    )
    key_raw_grad = (
        norm_back(key_raw, key_inv, key_gain, unrotate(key_grads, cosine_table, sine_table))
        .astype(jnp.bfloat16)
        .reshape(row_count, groups * head_width)
    )
    input_terms = (
        jnp.dot(query_raw_grad, w_query.T, preferred_element_type=jnp.float32)
        + jnp.dot(key_raw_grad, w_key.T, preferred_element_type=jnp.float32)
        + jnp.dot(value_grads, w_value.T, preferred_element_type=jnp.float32)
    )
    input_grad = lax.psum_scatter(
        input_terms.astype(jnp.bfloat16), "head", scatter_dimension=0, tiled=True
    )
    grad_columns = jnp.concatenate([query_raw_grad, key_raw_grad, value_grads], axis=1)

    def reduced_columns(columns):
        partner_columns = lax.ppermute(columns, "ctx", partner)
        pair_sum = rounded_term(my_rows, columns) + rounded_term(partner_rows, partner_columns)
        return torus_reduce_scatter(pair_sum, my_rank, rank_count).astype(jnp.bfloat16)

    summed = jnp.concatenate(
        [
            reduced_columns(query_raw_grad),
            reduced_columns(jnp.concatenate([key_raw_grad, value_grads], axis=1)),
        ],
        axis=1,
    )
    query_cols = head_count * head_width
    key_cols = groups * head_width
    return (
        attended.reshape(row_count, query_cols),
        input_grad,
        summed[:, :query_cols],
        summed[:, query_cols : query_cols + key_cols],
        summed[:, query_cols + key_cols :],
    )


def solution(mesh):
    in_specs = (
        P(("ctx", "head"), None),
        P(None, "head"),
        P(None, "head"),
        P(None, "head"),
        P(),
        P(),
        P("ctx"),
        P("ctx", "head"),
    )
    out_specs = (
        P("ctx", "head"),
        P(("ctx", "head"), None),
        P("ctx", "head"),
        P("ctx", "head"),
        P("ctx", "head"),
    )
    return jax.shard_map(
        on_device, mesh=mesh, in_specs=in_specs, out_specs=out_specs, check_vma=False
    )
```

```python
from functools import reduce
import math

import jax
import jax.numpy as jnp
from jax import lax
from jax.experimental import pallas as pl
from jax.experimental.pallas import tpu as pltpu
from jax.sharding import PartitionSpec as P

WINDOW = 1024


norm_eps = 1e-06
rope_base = 10000.0


def passed_along(block, axis, distance):
    devices = range(lax.axis_size(axis))
    route = [(i - distance, i) for i in devices if i - distance in devices]
    return lax.ppermute(block, axis, route)


CORES = 2
Y_CHIPS = 4


def ring_pairs(rank_count, along_y):
    z_chips = rank_count // (CORES * Y_CHIPS)
    forward = []
    for z in range(z_chips):
        for y in range(Y_CHIPS):
            for core in range(CORES):
                source = (z * Y_CHIPS + y) * CORES + core
                if along_y:
                    target = (z * Y_CHIPS + (y + 1) % Y_CHIPS) * CORES + core
                else:
                    target = (((z + 1) % z_chips) * Y_CHIPS + y) * CORES + core
                forward.append((source, target))
    backward = [(target, source) for source, target in forward]
    return forward, backward


def ring_reduce_scatter(parts, axis, position, forward, backward):
    count = parts.shape[axis]
    half = parts.shape[-1] // 2

    def own(index, low):
        piece = lax.slice_in_dim(parts, low, low + half, axis=parts.ndim - 1)
        return lax.dynamic_index_in_dim(piece, index % count, axis, keepdims=False)

    up = own(position + count - 1, 0)
    down = own(position + 1, half)
    for step in range(count - 1):
        up = lax.ppermute(up.astype(jnp.bfloat16), "ctx", forward).astype(jnp.float32) + own(
            position + 2 * count - step - 2, 0
        )
        down = lax.ppermute(down.astype(jnp.bfloat16), "ctx", backward).astype(
            jnp.float32
        ) + own(position + step + 2, half)
    return jnp.concatenate([up, down], axis=-1)


def pair_rows(gathered, core, rank_count):
    z_chips = rank_count // (CORES * Y_CHIPS)
    count, width = gathered.shape
    grid = gathered.reshape(count, z_chips, Y_CHIPS, CORES, width // rank_count)
    return lax.dynamic_index_in_dim(grid, core, 3, keepdims=False).reshape(count, width // CORES)


def rounded_term(rows, columns):
    return (
        lax.dot_general(rows, columns, (((0,), (0,)), ((), ())), preferred_element_type=jnp.float32)
        .astype(jnp.bfloat16)
        .astype(jnp.float32)
    )


def torus_reduce_scatter(pair_sum, my_rank, rank_count):
    z_chips = rank_count // (CORES * Y_CHIPS)
    rows, columns = pair_sum.shape
    y_pos = (my_rank // CORES) % Y_CHIPS
    z_pos = my_rank // (CORES * Y_CHIPS)
    grid = pair_sum.reshape(z_chips, Y_CHIPS, rows // (z_chips * Y_CHIPS), columns)
    y_forward, y_backward = ring_pairs(rank_count, True)
    z_forward, z_backward = ring_pairs(rank_count, False)
    half = columns // 2
    first = grid[..., :half]
    second = grid[..., half:]
    first = ring_reduce_scatter(first, 1, y_pos, y_forward, y_backward)
    first = ring_reduce_scatter(first, 0, z_pos, z_forward, z_backward)
    second = ring_reduce_scatter(second, 0, z_pos, z_forward, z_backward)
    second = ring_reduce_scatter(second, 0, y_pos, y_forward, y_backward)
    return jnp.concatenate([first, second], axis=-1)


def attention_body(q_ref, k_ref, v_ref, do_ref, lo_ref, att_ref, dq_ref, dk_ref, dv_ref):
    rows = q_ref.shape[0]
    keys, width = k_ref.shape
    k = k_ref[...]
    v = v_ref[...]
    key_index = lax.broadcasted_iota(jnp.int32, (rows, keys), 1)
    query_index = lax.broadcasted_iota(jnp.int32, (rows, keys), 0)
    visible = (key_index >= lo_ref[...]) & (key_index <= query_index + (keys - rows))
    dk = jnp.zeros((keys, width), jnp.float32)
    dv = jnp.zeros((keys, width), jnp.float32)
    for head in range(q_ref.shape[1] // width):
        cols = slice(head * width, (head + 1) * width)
        q = q_ref[:, cols]
        do = do_ref[:, cols]
        scores = lax.dot_general(q, k, (((1,), (1,)), ((), ())), preferred_element_type=jnp.float32)
        peak = jnp.max(jnp.where(visible, scores, -jnp.inf), axis=-1, keepdims=True)
        weights = jnp.where(visible, jnp.exp(scores - peak), 0.0)
        probs = weights / jnp.sum(weights, axis=-1, keepdims=True)
        probs_bf16 = probs.astype(jnp.bfloat16)
        attended = jnp.dot(probs_bf16, v, preferred_element_type=jnp.float32).astype(jnp.bfloat16)
        att_ref[:, cols] = attended
        delta = jnp.sum(
            do.astype(jnp.float32) * attended.astype(jnp.float32), axis=-1, keepdims=True
        )
        dprobs = lax.dot_general(do, v, (((1,), (1,)), ((), ())), preferred_element_type=jnp.float32)
        dscores = (probs * (dprobs - delta)).astype(jnp.bfloat16)
        dq_ref[:, cols] = jnp.dot(dscores, k, preferred_element_type=jnp.float32)
        dk = dk + lax.dot_general(
            dscores, q, (((0,), (0,)), ((), ())), preferred_element_type=jnp.float32
        )
        dv = dv + lax.dot_general(
            probs_bf16, do, (((0,), (0,)), ((), ())), preferred_element_type=jnp.float32
        )
    dk_ref[...] = dk
    dv_ref[...] = dv


def fused_attention(q2d, k_all, v_all, do2d, lower, groups):
    rows, query_cols = q2d.shape
    keys, kv_cols = k_all.shape
    width = kv_cols // groups
    per_group = query_cols // groups
    heads = query_cols // width
    flops = 2 * rows * keys * width * 6 * heads
    io_bytes = 2 * (3 * rows * query_cols + 2 * keys * kv_cols) + 4 * (rows * query_cols + 2 * keys * kv_cols)
    return pl.pallas_call(
        attention_body,
        grid=(groups,),
        in_specs=[
            pl.BlockSpec((rows, per_group), lambda g: (0, g)),
            pl.BlockSpec((keys, width), lambda g: (0, g)),
            pl.BlockSpec((keys, width), lambda g: (0, g)),
            pl.BlockSpec((rows, per_group), lambda g: (0, g)),
            pl.BlockSpec((rows, 1), lambda g: (0, 0)),
        ],
        out_specs=[
            pl.BlockSpec((rows, per_group), lambda g: (0, g)),
            pl.BlockSpec((rows, per_group), lambda g: (0, g)),
            pl.BlockSpec((keys, width), lambda g: (0, g)),
            pl.BlockSpec((keys, width), lambda g: (0, g)),
        ],
        out_shape=[
            jax.ShapeDtypeStruct((rows, query_cols), jnp.bfloat16),
            jax.ShapeDtypeStruct((rows, query_cols), jnp.float32),
            jax.ShapeDtypeStruct((keys, kv_cols), jnp.float32),
            jax.ShapeDtypeStruct((keys, kv_cols), jnp.float32),
        ],
        compiler_params=pltpu.CompilerParams(vmem_limit_bytes=56 * 1024 * 1024),
        cost_estimate=pl.CostEstimate(
            flops=flops, transcendentals=rows * keys * heads, bytes_accessed=io_bytes
        ),
    )(q2d, k_all, v_all, do2d, lower)


def rope_tables(positions, head_width):
    half_width = head_width // 2
    indices = jnp.arange(half_width, dtype=jnp.float32)
    frequency = jnp.power(rope_base, -2.0 * indices / head_width)
    angles = positions.astype(jnp.float32)[:, None] * frequency[None, :]
    return (jnp.cos(angles)[:, None, :], jnp.sin(angles)[:, None, :])


def rotate(vector, cosine_table, sine_table):
    half_width = vector.shape[-1] // 2
    lower_half = vector[..., :half_width]
    upper_half = vector[..., half_width:]
    return jnp.concatenate(
        [
            lower_half * cosine_table - upper_half * sine_table,
            upper_half * cosine_table + lower_half * sine_table,
        ],
        axis=-1,
    )


def unrotate(rotated, cosine_table, sine_table):
    half_width = rotated.shape[-1] // 2
    lower_half = rotated[..., :half_width]
    upper_half = rotated[..., half_width:]
    return jnp.concatenate(
        [
            lower_half * cosine_table + upper_half * sine_table,
            upper_half * cosine_table - lower_half * sine_table,
        ],
        axis=-1,
    )


def normalize(vector, gain_vector):
    inv_rms = lax.rsqrt(jnp.mean(vector * vector, axis=-1, keepdims=True) + norm_eps)
    return (vector * inv_rms * gain_vector, inv_rms)


def norm_back(vector, inv_rms, gain_vector, upstream):
    scaled = upstream * gain_vector
    return inv_rms * scaled - vector * (inv_rms * inv_rms * inv_rms) * jnp.mean(
        vector * scaled, axis=-1, keepdims=True
    )


def on_device(tokens, w_query, w_key, w_value, query_gain, key_gain, positions, out_grad):
    gathered = lax.all_gather(tokens, "head", axis=0, tiled=True)
    row_count = gathered.shape[0]
    head_width = query_gain.shape[0]
    head_count = w_query.shape[1] // head_width
    groups = w_key.shape[1] // head_width
    group_size = head_count // groups
    rank_count = lax.axis_size("ctx")
    my_rank = lax.axis_index("ctx")
    reach_blocks = min((WINDOW - 2) // row_count + 1, rank_count - 1)
    core = my_rank % CORES
    partner = [(rank, rank ^ 1) for rank in range(rank_count)]
    my_rows = pair_rows(gathered, core, rank_count)
    partner_rows = lax.ppermute(
        pair_rows(gathered, CORES - 1 - core, rank_count), "ctx", partner
    )
    query_scale = 1.0 / math.sqrt(head_width)
    query_raw = jnp.dot(gathered, w_query, preferred_element_type=jnp.float32).reshape(
        row_count, head_count, head_width
    )
    key_raw = jnp.dot(gathered, w_key, preferred_element_type=jnp.float32).reshape(
        row_count, groups, head_width
    )
    value_states = jnp.dot(gathered, w_value, preferred_element_type=jnp.float32).astype(
        jnp.bfloat16
    )
    cosine_table, sine_table = rope_tables(positions, head_width)
    query_normed, query_inv = normalize(query_raw, query_gain)
    key_normed, key_inv = normalize(key_raw, key_gain)
    query_states = (
        (rotate(query_normed, cosine_table, sine_table) * query_scale)
        .astype(jnp.bfloat16)
        .reshape(row_count, groups, group_size, head_width)
    )
    key_states = (
        rotate(key_normed, cosine_table, sine_table)
        .astype(jnp.bfloat16)
        .reshape(row_count, groups * head_width)
    )
    local_kv = jnp.stack([key_states, value_states])
    blocks = [local_kv] + [
        passed_along(local_kv, "ctx", stride) for stride in range(1, reach_blocks + 1)
    ]
    offsets = jnp.arange(row_count, dtype=jnp.int32)
    key_count = (reach_blocks + 1) * row_count
    lower = jnp.maximum(
        (reach_blocks - my_rank) * row_count,
        reach_blocks * row_count + offsets - jnp.minimum(positions, WINDOW - 1),
    )[:, None]
    ordered = blocks[::-1]
    all_keys = jnp.concatenate([block[0] for block in ordered], axis=0)
    all_values = jnp.concatenate([block[1] for block in ordered], axis=0)
    attended, query_grads, key_grad_all, value_grad_all = fused_attention(
        query_states.reshape(row_count, head_count * head_width),
        all_keys,
        all_values,
        out_grad,
        lower,
        groups,
    )

    def grad_rows(stride):
        start = key_count - (stride + 1) * row_count
        return jnp.stack(
            [
                key_grad_all[start : start + row_count],
                value_grad_all[start : start + row_count],
            ]
        )

    key_grad_parts = [grad_rows(stride) for stride in range(reach_blocks + 1)]
    returned = reduce(
        jnp.add,
        [key_grad_parts[0]]
        + [
            passed_along(key_grad_parts[stride].astype(jnp.bfloat16), "ctx", -stride).astype(
                jnp.float32
            )
            for stride in range(1, reach_blocks + 1)
        ],
    )
    key_grads = returned[0].reshape(row_count, groups, head_width)
    value_grads = returned[1].astype(jnp.bfloat16)
    query_raw_grad = (
        norm_back(
            query_raw,
            query_inv,
            query_gain,
            unrotate(
                query_grads.reshape(row_count, head_count, head_width), cosine_table, sine_table
            )
            * query_scale,
        )
        .astype(jnp.bfloat16)
        .reshape(row_count, head_count * head_width)
    )
    key_raw_grad = (
        norm_back(key_raw, key_inv, key_gain, unrotate(key_grads, cosine_table, sine_table))
        .astype(jnp.bfloat16)
        .reshape(row_count, groups * head_width)
    )
    input_terms = (
        jnp.dot(query_raw_grad, w_query.T, preferred_element_type=jnp.float32)
        + jnp.dot(key_raw_grad, w_key.T, preferred_element_type=jnp.float32)
        + jnp.dot(value_grads, w_value.T, preferred_element_type=jnp.float32)
    )
    input_grad = lax.psum_scatter(
        input_terms.astype(jnp.bfloat16), "head", scatter_dimension=0, tiled=True
    )
    grad_columns = jnp.concatenate([query_raw_grad, key_raw_grad, value_grads], axis=1)
    partner_columns = lax.ppermute(grad_columns, "ctx", partner)
    pair_sum = rounded_term(my_rows, grad_columns) + rounded_term(partner_rows, partner_columns)
    summed = torus_reduce_scatter(pair_sum, my_rank, rank_count).astype(jnp.bfloat16)
    query_cols = head_count * head_width
    key_cols = groups * head_width
    return (
        attended.reshape(row_count, query_cols),
        input_grad,
        summed[:, :query_cols],
        summed[:, query_cols : query_cols + key_cols],
        summed[:, query_cols + key_cols :],
    )


def solution(mesh):
    in_specs = (
        P(("ctx", "head"), None),
        P(None, "head"),
        P(None, "head"),
        P(None, "head"),
        P(),
        P(),
        P("ctx"),
        P("ctx", "head"),
    )
    out_specs = (
        P("ctx", "head"),
        P(("ctx", "head"), None),
        P("ctx", "head"),
        P("ctx", "head"),
        P("ctx", "head"),
    )
    return jax.shard_map(
        on_device, mesh=mesh, in_specs=in_specs, out_specs=out_specs, check_vma=False
    )
```

```python
from functools import reduce
import math

import jax
import jax.numpy as jnp
from jax import lax
from jax.experimental import pallas as pl
from jax.experimental.pallas import tpu as pltpu
from jax.sharding import PartitionSpec as P

WINDOW = 1024


norm_eps = 1e-06
rope_base = 10000.0


def passed_along(block, axis, distance):
    devices = range(lax.axis_size(axis))
    route = [(i - distance, i) for i in devices if i - distance in devices]
    return lax.ppermute(block, axis, route)


CORES = 2
Y_CHIPS = 4


def ring_pairs(rank_count, along_y):
    z_chips = rank_count // (CORES * Y_CHIPS)
    forward = []
    for z in range(z_chips):
        for y in range(Y_CHIPS):
            for core in range(CORES):
                source = (z * Y_CHIPS + y) * CORES + core
                if along_y:
                    target = (z * Y_CHIPS + (y + 1) % Y_CHIPS) * CORES + core
                else:
                    target = (((z + 1) % z_chips) * Y_CHIPS + y) * CORES + core
                forward.append((source, target))
    backward = [(target, source) for source, target in forward]
    return forward, backward


def ring_reduce_scatter(parts, axis, position, forward, backward):
    count = parts.shape[axis]
    half = parts.shape[-1] // 2

    def own(index, low):
        piece = lax.slice_in_dim(parts, low, low + half, axis=parts.ndim - 1)
        return lax.dynamic_index_in_dim(piece, index % count, axis, keepdims=False)

    up = own(position + count - 1, 0)
    down = own(position + 1, half)
    for step in range(count - 1):
        up = lax.ppermute(up.astype(jnp.bfloat16), "ctx", forward).astype(jnp.float32) + own(
            position + 2 * count - step - 2, 0
        )
        down = lax.ppermute(down.astype(jnp.bfloat16), "ctx", backward).astype(
            jnp.float32
        ) + own(position + step + 2, half)
    return jnp.concatenate([up, down], axis=-1)


def ring_gather(block, axis):
    count = lax.axis_size(axis)
    if count != 4:
        return lax.all_gather(block, axis, axis=0, tiled=True)
    position = lax.axis_index(axis)
    up_pairs = [(i, (i + 1) % count) for i in range(count)]
    down_pairs = [(i, (i - 1) % count) for i in range(count)]
    half = block.shape[1] // 2
    from_below = lax.ppermute(block, axis, up_pairs)
    from_above = lax.ppermute(block, axis, down_pairs)
    opposite = jnp.concatenate(
        [
            lax.ppermute(from_below[:, :half], axis, up_pairs),
            lax.ppermute(from_above[:, half:], axis, down_pairs),
        ],
        axis=1,
    )
    relative = jnp.concatenate([block, from_above, opposite, from_below], axis=0)
    doubled = jnp.concatenate([relative, relative], axis=0)
    rows = block.shape[0]
    start = (count - position) % count * rows
    return lax.dynamic_slice_in_dim(doubled, start, count * rows, axis=0)


def pair_rows(gathered, core, rank_count):
    z_chips = rank_count // (CORES * Y_CHIPS)
    count, width = gathered.shape
    grid = gathered.reshape(count, z_chips, Y_CHIPS, CORES, width // rank_count)
    return lax.dynamic_index_in_dim(grid, core, 3, keepdims=False).reshape(count, width // CORES)


def rounded_term(rows, columns):
    return (
        lax.dot_general(rows, columns, (((0,), (0,)), ((), ())), preferred_element_type=jnp.float32)
        .astype(jnp.bfloat16)
        .astype(jnp.float32)
    )


def torus_reduce_scatter(pair_sum, my_rank, rank_count):
    z_chips = rank_count // (CORES * Y_CHIPS)
    rows, columns = pair_sum.shape
    y_pos = (my_rank // CORES) % Y_CHIPS
    z_pos = my_rank // (CORES * Y_CHIPS)
    grid = pair_sum.reshape(z_chips, Y_CHIPS, rows // (z_chips * Y_CHIPS), columns)
    y_forward, y_backward = ring_pairs(rank_count, True)
    z_forward, z_backward = ring_pairs(rank_count, False)
    half = columns // 2
    first = grid[..., :half]
    second = grid[..., half:]
    first = ring_reduce_scatter(first, 1, y_pos, y_forward, y_backward)
    first = ring_reduce_scatter(first, 0, z_pos, z_forward, z_backward)
    second = ring_reduce_scatter(second, 0, z_pos, z_forward, z_backward)
    second = ring_reduce_scatter(second, 0, y_pos, y_forward, y_backward)
    return jnp.concatenate([first, second], axis=-1)


def attention_body(q_ref, k_ref, v_ref, do_ref, lo_ref, att_ref, dq_ref, dk_ref, dv_ref):
    rows = q_ref.shape[0]
    keys, width = k_ref.shape
    k = k_ref[...]
    v = v_ref[...]
    key_index = lax.broadcasted_iota(jnp.int32, (rows, keys), 1)
    query_index = lax.broadcasted_iota(jnp.int32, (rows, keys), 0)
    visible = (key_index >= lo_ref[...]) & (key_index <= query_index + (keys - rows))
    dk = jnp.zeros((keys, width), jnp.float32)
    dv = jnp.zeros((keys, width), jnp.float32)
    for head in range(q_ref.shape[1] // width):
        cols = slice(head * width, (head + 1) * width)
        q = q_ref[:, cols]
        do = do_ref[:, cols]
        scores = lax.dot_general(q, k, (((1,), (1,)), ((), ())), preferred_element_type=jnp.float32)
        peak = jnp.max(jnp.where(visible, scores, -jnp.inf), axis=-1, keepdims=True)
        weights = jnp.where(visible, jnp.exp(scores - peak), 0.0)
        probs = weights / jnp.sum(weights, axis=-1, keepdims=True)
        probs_bf16 = probs.astype(jnp.bfloat16)
        attended = jnp.dot(probs_bf16, v, preferred_element_type=jnp.float32).astype(jnp.bfloat16)
        att_ref[:, cols] = attended
        delta = jnp.sum(
            do.astype(jnp.float32) * attended.astype(jnp.float32), axis=-1, keepdims=True
        )
        dprobs = lax.dot_general(do, v, (((1,), (1,)), ((), ())), preferred_element_type=jnp.float32)
        dscores = (probs * (dprobs - delta)).astype(jnp.bfloat16)
        dq_ref[:, cols] = jnp.dot(dscores, k, preferred_element_type=jnp.float32)
        dk = dk + lax.dot_general(
            dscores, q, (((0,), (0,)), ((), ())), preferred_element_type=jnp.float32
        )
        dv = dv + lax.dot_general(
            probs_bf16, do, (((0,), (0,)), ((), ())), preferred_element_type=jnp.float32
        )
    dk_ref[...] = dk
    dv_ref[...] = dv


def fused_attention(q2d, k_all, v_all, do2d, lower, groups):
    rows, query_cols = q2d.shape
    keys, kv_cols = k_all.shape
    width = kv_cols // groups
    per_group = query_cols // groups
    heads = query_cols // width
    flops = 2 * rows * keys * width * 6 * heads
    io_bytes = 2 * (3 * rows * query_cols + 2 * keys * kv_cols) + 4 * (rows * query_cols + 2 * keys * kv_cols)
    return pl.pallas_call(
        attention_body,
        grid=(groups,),
        in_specs=[
            pl.BlockSpec((rows, per_group), lambda g: (0, g)),
            pl.BlockSpec((keys, width), lambda g: (0, g)),
            pl.BlockSpec((keys, width), lambda g: (0, g)),
            pl.BlockSpec((rows, per_group), lambda g: (0, g)),
            pl.BlockSpec((rows, 1), lambda g: (0, 0)),
        ],
        out_specs=[
            pl.BlockSpec((rows, per_group), lambda g: (0, g)),
            pl.BlockSpec((rows, per_group), lambda g: (0, g)),
            pl.BlockSpec((keys, width), lambda g: (0, g)),
            pl.BlockSpec((keys, width), lambda g: (0, g)),
        ],
        out_shape=[
            jax.ShapeDtypeStruct((rows, query_cols), jnp.bfloat16),
            jax.ShapeDtypeStruct((rows, query_cols), jnp.float32),
            jax.ShapeDtypeStruct((keys, kv_cols), jnp.float32),
            jax.ShapeDtypeStruct((keys, kv_cols), jnp.float32),
        ],
        compiler_params=pltpu.CompilerParams(vmem_limit_bytes=56 * 1024 * 1024),
        cost_estimate=pl.CostEstimate(
            flops=flops, transcendentals=rows * keys * heads, bytes_accessed=io_bytes
        ),
    )(q2d, k_all, v_all, do2d, lower)


def rope_tables(positions, head_width):
    half_width = head_width // 2
    indices = jnp.arange(half_width, dtype=jnp.float32)
    frequency = jnp.power(rope_base, -2.0 * indices / head_width)
    angles = positions.astype(jnp.float32)[:, None] * frequency[None, :]
    return (jnp.cos(angles)[:, None, :], jnp.sin(angles)[:, None, :])


def rotate(vector, cosine_table, sine_table):
    half_width = vector.shape[-1] // 2
    lower_half = vector[..., :half_width]
    upper_half = vector[..., half_width:]
    return jnp.concatenate(
        [
            lower_half * cosine_table - upper_half * sine_table,
            upper_half * cosine_table + lower_half * sine_table,
        ],
        axis=-1,
    )


def unrotate(rotated, cosine_table, sine_table):
    half_width = rotated.shape[-1] // 2
    lower_half = rotated[..., :half_width]
    upper_half = rotated[..., half_width:]
    return jnp.concatenate(
        [
            lower_half * cosine_table + upper_half * sine_table,
            upper_half * cosine_table - lower_half * sine_table,
        ],
        axis=-1,
    )


def normalize(vector, gain_vector):
    inv_rms = lax.rsqrt(jnp.mean(vector * vector, axis=-1, keepdims=True) + norm_eps)
    return (vector * inv_rms * gain_vector, inv_rms)


def norm_back(vector, inv_rms, gain_vector, upstream):
    scaled = upstream * gain_vector
    return inv_rms * scaled - vector * (inv_rms * inv_rms * inv_rms) * jnp.mean(
        vector * scaled, axis=-1, keepdims=True
    )


def on_device(tokens, w_query, w_key, w_value, query_gain, key_gain, positions, out_grad):
    gathered = ring_gather(tokens, "head")
    row_count = gathered.shape[0]
    head_width = query_gain.shape[0]
    head_count = w_query.shape[1] // head_width
    groups = w_key.shape[1] // head_width
    group_size = head_count // groups
    rank_count = lax.axis_size("ctx")
    my_rank = lax.axis_index("ctx")
    reach_blocks = min((WINDOW - 2) // row_count + 1, rank_count - 1)
    core = my_rank % CORES
    partner = [(rank, rank ^ 1) for rank in range(rank_count)]
    my_rows = pair_rows(gathered, core, rank_count)
    partner_rows = lax.ppermute(
        pair_rows(gathered, CORES - 1 - core, rank_count), "ctx", partner
    )
    query_scale = 1.0 / math.sqrt(head_width)
    query_raw = jnp.dot(gathered, w_query, preferred_element_type=jnp.float32).reshape(
        row_count, head_count, head_width
    )
    key_raw = jnp.dot(gathered, w_key, preferred_element_type=jnp.float32).reshape(
        row_count, groups, head_width
    )
    value_states = jnp.dot(gathered, w_value, preferred_element_type=jnp.float32).astype(
        jnp.bfloat16
    )
    cosine_table, sine_table = rope_tables(positions, head_width)
    query_normed, query_inv = normalize(query_raw, query_gain)
    key_normed, key_inv = normalize(key_raw, key_gain)
    query_states = (
        (rotate(query_normed, cosine_table, sine_table) * query_scale)
        .astype(jnp.bfloat16)
        .reshape(row_count, groups, group_size, head_width)
    )
    key_states = (
        rotate(key_normed, cosine_table, sine_table)
        .astype(jnp.bfloat16)
        .reshape(row_count, groups * head_width)
    )
    local_kv = jnp.stack([key_states, value_states])
    blocks = [local_kv] + [
        passed_along(local_kv, "ctx", stride) for stride in range(1, reach_blocks + 1)
    ]
    offsets = jnp.arange(row_count, dtype=jnp.int32)
    key_count = (reach_blocks + 1) * row_count
    lower = jnp.maximum(
        (reach_blocks - my_rank) * row_count,
        reach_blocks * row_count + offsets - jnp.minimum(positions, WINDOW - 1),
    )[:, None]
    ordered = blocks[::-1]
    all_keys = jnp.concatenate([block[0] for block in ordered], axis=0)
    all_values = jnp.concatenate([block[1] for block in ordered], axis=0)
    attended, query_grads, key_grad_all, value_grad_all = fused_attention(
        query_states.reshape(row_count, head_count * head_width),
        all_keys,
        all_values,
        out_grad,
        lower,
        groups,
    )

    def grad_rows(stride):
        start = key_count - (stride + 1) * row_count
        return jnp.stack(
            [
                key_grad_all[start : start + row_count],
                value_grad_all[start : start + row_count],
            ]
        )

    key_grad_parts = [grad_rows(stride) for stride in range(reach_blocks + 1)]
    returned = reduce(
        jnp.add,
        [key_grad_parts[0]]
        + [
            passed_along(key_grad_parts[stride].astype(jnp.bfloat16), "ctx", -stride).astype(
                jnp.float32
            )
            for stride in range(1, reach_blocks + 1)
        ],
    )
    key_grads = returned[0].reshape(row_count, groups, head_width)
    value_grads = returned[1].astype(jnp.bfloat16)
    query_raw_grad = (
        norm_back(
            query_raw,
            query_inv,
            query_gain,
            unrotate(
                query_grads.reshape(row_count, head_count, head_width), cosine_table, sine_table
            )
            * query_scale,
        )
        .astype(jnp.bfloat16)
        .reshape(row_count, head_count * head_width)
    )
    key_raw_grad = (
        norm_back(key_raw, key_inv, key_gain, unrotate(key_grads, cosine_table, sine_table))
        .astype(jnp.bfloat16)
        .reshape(row_count, groups * head_width)
    )
    input_terms = (
        jnp.dot(query_raw_grad, w_query.T, preferred_element_type=jnp.float32)
        + jnp.dot(key_raw_grad, w_key.T, preferred_element_type=jnp.float32)
        + jnp.dot(value_grads, w_value.T, preferred_element_type=jnp.float32)
    )
    input_grad = lax.psum_scatter(
        input_terms.astype(jnp.bfloat16), "head", scatter_dimension=0, tiled=True
    )
    grad_columns = jnp.concatenate([query_raw_grad, key_raw_grad, value_grads], axis=1)
    partner_columns = lax.ppermute(grad_columns, "ctx", partner)
    pair_sum = rounded_term(my_rows, grad_columns) + rounded_term(partner_rows, partner_columns)
    summed = torus_reduce_scatter(pair_sum, my_rank, rank_count).astype(jnp.bfloat16)
    query_cols = head_count * head_width
    key_cols = groups * head_width
    return (
        attended.reshape(row_count, query_cols),
        input_grad,
        summed[:, :query_cols],
        summed[:, query_cols : query_cols + key_cols],
        summed[:, query_cols + key_cols :],
    )


def solution(mesh):
    in_specs = (
        P(("ctx", "head"), None),
        P(None, "head"),
        P(None, "head"),
        P(None, "head"),
        P(),
        P(),
        P("ctx"),
        P("ctx", "head"),
    )
    out_specs = (
        P("ctx", "head"),
        P(("ctx", "head"), None),
        P("ctx", "head"),
        P("ctx", "head"),
        P("ctx", "head"),
    )
    return jax.shard_map(
        on_device, mesh=mesh, in_specs=in_specs, out_specs=out_specs, check_vma=False
    )
```

```python
from functools import reduce
import math

import jax
import jax.numpy as jnp
from jax import lax
from jax.experimental import pallas as pl
from jax.experimental.pallas import tpu as pltpu
from jax.sharding import PartitionSpec as P

WINDOW = 1024


norm_eps = 1e-06
rope_base = 10000.0


def passed_along(block, axis, distance):
    devices = range(lax.axis_size(axis))
    route = [(i - distance, i) for i in devices if i - distance in devices]
    return lax.ppermute(block, axis, route)


CORES = 2
Y_CHIPS = 4


def ring_pairs(rank_count, along_y):
    z_chips = rank_count // (CORES * Y_CHIPS)
    forward = []
    for z in range(z_chips):
        for y in range(Y_CHIPS):
            for core in range(CORES):
                source = (z * Y_CHIPS + y) * CORES + core
                if along_y:
                    target = (z * Y_CHIPS + (y + 1) % Y_CHIPS) * CORES + core
                else:
                    target = (((z + 1) % z_chips) * Y_CHIPS + y) * CORES + core
                forward.append((source, target))
    backward = [(target, source) for source, target in forward]
    return forward, backward


def ring_reduce_scatter(parts, axis, position, forward, backward):
    count = parts.shape[axis]
    half = parts.shape[-1] // 2

    def own(index, low):
        piece = lax.slice_in_dim(parts, low, low + half, axis=parts.ndim - 1)
        return lax.dynamic_index_in_dim(piece, index % count, axis, keepdims=False)

    up = own(position + count - 1, 0)
    down = own(position + 1, half)
    for step in range(count - 1):
        up = lax.ppermute(up.astype(jnp.bfloat16), "ctx", forward).astype(jnp.float32) + own(
            position + 2 * count - step - 2, 0
        )
        down = lax.ppermute(down.astype(jnp.bfloat16), "ctx", backward).astype(
            jnp.float32
        ) + own(position + step + 2, half)
    return jnp.concatenate([up, down], axis=-1)


def pair_rows(gathered, core, rank_count):
    z_chips = rank_count // (CORES * Y_CHIPS)
    count, width = gathered.shape
    grid = gathered.reshape(count, z_chips, Y_CHIPS, CORES, width // rank_count)
    return lax.dynamic_index_in_dim(grid, core, 3, keepdims=False).reshape(count, width // CORES)


def rounded_term(rows, columns):
    return (
        lax.dot_general(rows, columns, (((0,), (0,)), ((), ())), preferred_element_type=jnp.float32)
        .astype(jnp.bfloat16)
        .astype(jnp.float32)
    )


def torus_reduce_scatter(pair_sum, my_rank, rank_count):
    z_chips = rank_count // (CORES * Y_CHIPS)
    rows, columns = pair_sum.shape
    y_pos = (my_rank // CORES) % Y_CHIPS
    z_pos = my_rank // (CORES * Y_CHIPS)
    grid = pair_sum.reshape(z_chips, Y_CHIPS, rows // (z_chips * Y_CHIPS), columns)
    y_forward, y_backward = ring_pairs(rank_count, True)
    z_forward, z_backward = ring_pairs(rank_count, False)
    half = columns // 2
    first = grid[..., :half]
    second = grid[..., half:]
    first = ring_reduce_scatter(first, 1, y_pos, y_forward, y_backward)
    first = ring_reduce_scatter(first, 0, z_pos, z_forward, z_backward)
    second = ring_reduce_scatter(second, 0, z_pos, z_forward, z_backward)
    second = ring_reduce_scatter(second, 0, y_pos, y_forward, y_backward)
    return jnp.concatenate([first, second], axis=-1)


def attention_body(q_ref, k_ref, v_ref, do_ref, lo_ref, att_ref, dq_ref, dk_ref, dv_ref):
    rows = q_ref.shape[0]
    keys, width = k_ref.shape
    k = k_ref[...]
    v = v_ref[...]
    key_index = lax.broadcasted_iota(jnp.int32, (rows, keys), 1)
    query_index = lax.broadcasted_iota(jnp.int32, (rows, keys), 0)
    visible = (key_index >= lo_ref[...]) & (key_index <= query_index + (keys - rows))
    dk = jnp.zeros((keys, width), jnp.float32)
    dv = jnp.zeros((keys, width), jnp.float32)
    for head in range(q_ref.shape[1] // width):
        cols = slice(head * width, (head + 1) * width)
        q = q_ref[:, cols]
        do = do_ref[:, cols]
        scores = lax.dot_general(q, k, (((1,), (1,)), ((), ())), preferred_element_type=jnp.float32)
        peak = jnp.max(jnp.where(visible, scores, -jnp.inf), axis=-1, keepdims=True)
        weights = jnp.where(visible, jnp.exp(scores - peak), 0.0)
        probs = weights / jnp.sum(weights, axis=-1, keepdims=True)
        probs_bf16 = probs.astype(jnp.bfloat16)
        attended = jnp.dot(probs_bf16, v, preferred_element_type=jnp.float32).astype(jnp.bfloat16)
        att_ref[:, cols] = attended
        delta = jnp.sum(
            do.astype(jnp.float32) * attended.astype(jnp.float32), axis=-1, keepdims=True
        )
        dprobs = lax.dot_general(do, v, (((1,), (1,)), ((), ())), preferred_element_type=jnp.float32)
        dscores = (probs * (dprobs - delta)).astype(jnp.bfloat16)
        dq_ref[:, cols] = jnp.dot(dscores, k, preferred_element_type=jnp.float32)
        dk = dk + lax.dot_general(
            dscores, q, (((0,), (0,)), ((), ())), preferred_element_type=jnp.float32
        )
        dv = dv + lax.dot_general(
            probs_bf16, do, (((0,), (0,)), ((), ())), preferred_element_type=jnp.float32
        )
    dk_ref[...] = dk
    dv_ref[...] = dv


def fused_attention(q2d, k_all, v_all, do2d, lower, groups):
    rows, query_cols = q2d.shape
    keys, kv_cols = k_all.shape
    width = kv_cols // groups
    per_group = query_cols // groups
    heads = query_cols // width
    flops = 2 * rows * keys * width * 6 * heads
    io_bytes = 2 * (3 * rows * query_cols + 2 * keys * kv_cols) + 4 * (rows * query_cols + 2 * keys * kv_cols)
    return pl.pallas_call(
        attention_body,
        grid=(groups,),
        in_specs=[
            pl.BlockSpec((rows, per_group), lambda g: (0, g)),
            pl.BlockSpec((keys, width), lambda g: (0, g)),
            pl.BlockSpec((keys, width), lambda g: (0, g)),
            pl.BlockSpec((rows, per_group), lambda g: (0, g)),
            pl.BlockSpec((rows, 1), lambda g: (0, 0)),
        ],
        out_specs=[
            pl.BlockSpec((rows, per_group), lambda g: (0, g)),
            pl.BlockSpec((rows, per_group), lambda g: (0, g)),
            pl.BlockSpec((keys, width), lambda g: (0, g)),
            pl.BlockSpec((keys, width), lambda g: (0, g)),
        ],
        out_shape=[
            jax.ShapeDtypeStruct((rows, query_cols), jnp.bfloat16),
            jax.ShapeDtypeStruct((rows, query_cols), jnp.float32),
            jax.ShapeDtypeStruct((keys, kv_cols), jnp.float32),
            jax.ShapeDtypeStruct((keys, kv_cols), jnp.float32),
        ],
        compiler_params=pltpu.CompilerParams(vmem_limit_bytes=56 * 1024 * 1024),
        cost_estimate=pl.CostEstimate(
            flops=flops, transcendentals=rows * keys * heads, bytes_accessed=io_bytes
        ),
    )(q2d, k_all, v_all, do2d, lower)


def rope_tables(positions, head_width):
    half_width = head_width // 2
    indices = jnp.arange(half_width, dtype=jnp.float32)
    frequency = jnp.power(rope_base, -2.0 * indices / head_width)
    angles = positions.astype(jnp.float32)[:, None] * frequency[None, :]
    return (jnp.cos(angles)[:, None, :], jnp.sin(angles)[:, None, :])


def rotate(vector, cosine_table, sine_table):
    half_width = vector.shape[-1] // 2
    lower_half = vector[..., :half_width]
    upper_half = vector[..., half_width:]
    return jnp.concatenate(
        [
            lower_half * cosine_table - upper_half * sine_table,
            upper_half * cosine_table + lower_half * sine_table,
        ],
        axis=-1,
    )


def unrotate(rotated, cosine_table, sine_table):
    half_width = rotated.shape[-1] // 2
    lower_half = rotated[..., :half_width]
    upper_half = rotated[..., half_width:]
    return jnp.concatenate(
        [
            lower_half * cosine_table + upper_half * sine_table,
            upper_half * cosine_table - lower_half * sine_table,
        ],
        axis=-1,
    )


def normalize(vector, gain_vector):
    inv_rms = lax.rsqrt(jnp.mean(vector * vector, axis=-1, keepdims=True) + norm_eps)
    return (vector * inv_rms * gain_vector, inv_rms)


def norm_back(vector, inv_rms, gain_vector, upstream):
    scaled = upstream * gain_vector
    return inv_rms * scaled - vector * (inv_rms * inv_rms * inv_rms) * jnp.mean(
        vector * scaled, axis=-1, keepdims=True
    )


def on_device(tokens, w_query, w_key, w_value, query_gain, key_gain, positions, out_grad):
    gathered = lax.all_gather(tokens, "head", axis=0, tiled=True)
    row_count = gathered.shape[0]
    head_width = query_gain.shape[0]
    head_count = w_query.shape[1] // head_width
    groups = w_key.shape[1] // head_width
    group_size = head_count // groups
    rank_count = lax.axis_size("ctx")
    my_rank = lax.axis_index("ctx")
    reach_blocks = min((WINDOW - 2) // row_count + 1, rank_count - 1)
    core = my_rank % CORES
    partner = [(rank, rank ^ 1) for rank in range(rank_count)]
    my_rows = pair_rows(gathered, core, rank_count)
    partner_rows = lax.ppermute(
        pair_rows(gathered, CORES - 1 - core, rank_count), "ctx", partner
    )
    query_scale = 1.0 / math.sqrt(head_width)
    query_raw = jnp.dot(gathered, w_query, preferred_element_type=jnp.float32).reshape(
        row_count, head_count, head_width
    )
    key_raw = jnp.dot(gathered, w_key, preferred_element_type=jnp.float32).reshape(
        row_count, groups, head_width
    )
    value_states = jnp.dot(gathered, w_value, preferred_element_type=jnp.float32).astype(
        jnp.bfloat16
    )
    cosine_table, sine_table = rope_tables(positions, head_width)
    query_normed, query_inv = normalize(query_raw, query_gain)
    key_normed, key_inv = normalize(key_raw, key_gain)
    query_states = (
        (rotate(query_normed, cosine_table, sine_table) * query_scale)
        .astype(jnp.bfloat16)
        .reshape(row_count, groups, group_size, head_width)
    )
    key_states = (
        rotate(key_normed, cosine_table, sine_table)
        .astype(jnp.bfloat16)
        .reshape(row_count, groups * head_width)
    )
    local_kv = jnp.stack([key_states, value_states])
    blocks = [local_kv] + [
        passed_along(local_kv, "ctx", stride) for stride in range(1, reach_blocks + 1)
    ]
    offsets = jnp.arange(row_count, dtype=jnp.int32)
    key_count = (reach_blocks + 1) * row_count
    lower = jnp.maximum(
        (reach_blocks - my_rank) * row_count,
        reach_blocks * row_count + offsets - jnp.minimum(positions, WINDOW - 1),
    )[:, None]
    ordered = blocks[::-1]
    all_keys = jnp.concatenate([block[0] for block in ordered], axis=0)
    all_values = jnp.concatenate([block[1] for block in ordered], axis=0)
    attended, query_grads, key_grad_all, value_grad_all = fused_attention(
        query_states.reshape(row_count, head_count * head_width),
        all_keys,
        all_values,
        out_grad,
        lower,
        groups,
    )

    def grad_rows(stride):
        start = key_count - (stride + 1) * row_count
        return jnp.stack(
            [
                key_grad_all[start : start + row_count],
                value_grad_all[start : start + row_count],
            ]
        )

    key_grad_parts = [grad_rows(stride) for stride in range(reach_blocks + 1)]
    returned = reduce(
        jnp.add,
        [key_grad_parts[0]]
        + [
            passed_along(key_grad_parts[stride].astype(jnp.bfloat16), "ctx", -stride).astype(
                jnp.float32
            )
            for stride in range(1, reach_blocks + 1)
        ],
    )
    key_grads = returned[0].reshape(row_count, groups, head_width)
    value_grads = returned[1].astype(jnp.bfloat16)
    query_raw_grad = (
        norm_back(
            query_raw,
            query_inv,
            query_gain,
            unrotate(
                query_grads.reshape(row_count, head_count, head_width), cosine_table, sine_table
            )
            * query_scale,
        )
        .astype(jnp.bfloat16)
        .reshape(row_count, head_count * head_width)
    )
    key_raw_grad = (
        norm_back(key_raw, key_inv, key_gain, unrotate(key_grads, cosine_table, sine_table))
        .astype(jnp.bfloat16)
        .reshape(row_count, groups * head_width)
    )
    grad_columns = jnp.concatenate([query_raw_grad, key_raw_grad, value_grads], axis=1)
    partner_columns = lax.ppermute(grad_columns, "ctx", partner)
    pair_sum = rounded_term(my_rows, grad_columns) + rounded_term(partner_rows, partner_columns)
    pair_sum, query_raw_grad, key_raw_grad, value_grads = lax.optimization_barrier(
        (pair_sum, query_raw_grad, key_raw_grad, value_grads)
    )
    summed = torus_reduce_scatter(pair_sum, my_rank, rank_count).astype(jnp.bfloat16)
    input_terms = (
        jnp.dot(query_raw_grad, w_query.T, preferred_element_type=jnp.float32)
        + jnp.dot(key_raw_grad, w_key.T, preferred_element_type=jnp.float32)
        + jnp.dot(value_grads, w_value.T, preferred_element_type=jnp.float32)
    )
    input_grad = lax.psum_scatter(
        input_terms.astype(jnp.bfloat16), "head", scatter_dimension=0, tiled=True
    )
    query_cols = head_count * head_width
    key_cols = groups * head_width
    return (
        attended.reshape(row_count, query_cols),
        input_grad,
        summed[:, :query_cols],
        summed[:, query_cols : query_cols + key_cols],
        summed[:, query_cols + key_cols :],
    )


def solution(mesh):
    in_specs = (
        P(("ctx", "head"), None),
        P(None, "head"),
        P(None, "head"),
        P(None, "head"),
        P(),
        P(),
        P("ctx"),
        P("ctx", "head"),
    )
    out_specs = (
        P("ctx", "head"),
        P(("ctx", "head"), None),
        P("ctx", "head"),
        P("ctx", "head"),
        P("ctx", "head"),
    )
    return jax.shard_map(
        on_device, mesh=mesh, in_specs=in_specs, out_specs=out_specs, check_vma=False
    )
```

```python
from functools import reduce
import math

import jax
import jax.numpy as jnp
from jax import lax
from jax.experimental import pallas as pl
from jax.experimental.pallas import tpu as pltpu
from jax.sharding import PartitionSpec as P

WINDOW = 1024


norm_eps = 1e-06
rope_base = 10000.0


def passed_along(block, axis, distance):
    devices = range(lax.axis_size(axis))
    route = [(i - distance, i) for i in devices if i - distance in devices]
    return lax.ppermute(block, axis, route)


CORES = 2
Y_CHIPS = 4


def ring_pairs(rank_count, along_y):
    z_chips = rank_count // (CORES * Y_CHIPS)
    forward = []
    for z in range(z_chips):
        for y in range(Y_CHIPS):
            for core in range(CORES):
                source = (z * Y_CHIPS + y) * CORES + core
                if along_y:
                    target = (z * Y_CHIPS + (y + 1) % Y_CHIPS) * CORES + core
                else:
                    target = (((z + 1) % z_chips) * Y_CHIPS + y) * CORES + core
                forward.append((source, target))
    backward = [(target, source) for source, target in forward]
    return forward, backward


def ring_reduce_scatter(parts, axis, position, forward, backward):
    count = parts.shape[axis]
    half = parts.shape[-1] // 2

    def own(index, low):
        piece = lax.slice_in_dim(parts, low, low + half, axis=parts.ndim - 1)
        return lax.dynamic_index_in_dim(piece, index % count, axis, keepdims=False)

    up = own(position + count - 1, 0)
    down = own(position + 1, half)
    for step in range(count - 1):
        up = lax.ppermute(up.astype(jnp.bfloat16), "ctx", forward).astype(jnp.float32) + own(
            position + 2 * count - step - 2, 0
        )
        down = lax.ppermute(down.astype(jnp.bfloat16), "ctx", backward).astype(
            jnp.float32
        ) + own(position + step + 2, half)
    return jnp.concatenate([up, down], axis=-1)


def pair_rows(gathered, core, rank_count):
    z_chips = rank_count // (CORES * Y_CHIPS)
    count, width = gathered.shape
    grid = gathered.reshape(count, z_chips, Y_CHIPS, CORES, width // rank_count)
    return lax.dynamic_index_in_dim(grid, core, 3, keepdims=False).reshape(count, width // CORES)


def rounded_term(rows, columns):
    return (
        lax.dot_general(rows, columns, (((0,), (0,)), ((), ())), preferred_element_type=jnp.float32)
        .astype(jnp.bfloat16)
        .astype(jnp.float32)
    )


def torus_reduce_scatter(pair_sum, my_rank, rank_count):
    z_chips = rank_count // (CORES * Y_CHIPS)
    rows, columns = pair_sum.shape
    y_pos = (my_rank // CORES) % Y_CHIPS
    z_pos = my_rank // (CORES * Y_CHIPS)
    grid = pair_sum.reshape(z_chips, Y_CHIPS, rows // (z_chips * Y_CHIPS), columns)
    y_forward, y_backward = ring_pairs(rank_count, True)
    z_forward, z_backward = ring_pairs(rank_count, False)
    half = columns // 2
    first = grid[..., :half]
    second = grid[..., half:]
    first = ring_reduce_scatter(first, 1, y_pos, y_forward, y_backward)
    first = ring_reduce_scatter(first, 0, z_pos, z_forward, z_backward)
    second = ring_reduce_scatter(second, 0, z_pos, z_forward, z_backward)
    second = ring_reduce_scatter(second, 0, y_pos, y_forward, y_backward)
    return jnp.concatenate([first, second], axis=-1)


def attention_body(q_ref, k_ref, v_ref, do_ref, lo_ref, att_ref, dq_ref, dk_ref, dv_ref):
    rows = q_ref.shape[0]
    keys, width = k_ref.shape
    k = k_ref[...]
    v = v_ref[...]
    key_index = lax.broadcasted_iota(jnp.int32, (rows, keys), 1)
    query_index = lax.broadcasted_iota(jnp.int32, (rows, keys), 0)
    visible = (key_index >= lo_ref[...]) & (key_index <= query_index + (keys - rows))
    dk = jnp.zeros((keys, width), jnp.float32)
    dv = jnp.zeros((keys, width), jnp.float32)
    for head in range(q_ref.shape[1] // width):
        cols = slice(head * width, (head + 1) * width)
        q = q_ref[:, cols]
        do = do_ref[:, cols]
        scores = lax.dot_general(q, k, (((1,), (1,)), ((), ())), preferred_element_type=jnp.float32)
        peak = jnp.max(jnp.where(visible, scores, -jnp.inf), axis=-1, keepdims=True)
        weights = jnp.where(visible, jnp.exp(scores - peak), 0.0)
        probs = weights / jnp.sum(weights, axis=-1, keepdims=True)
        probs_bf16 = probs.astype(jnp.bfloat16)
        attended = jnp.dot(probs_bf16, v, preferred_element_type=jnp.float32).astype(jnp.bfloat16)
        att_ref[:, cols] = attended
        delta = jnp.sum(
            do.astype(jnp.float32) * attended.astype(jnp.float32), axis=-1, keepdims=True
        )
        dprobs = lax.dot_general(do, v, (((1,), (1,)), ((), ())), preferred_element_type=jnp.float32)
        dscores = (probs * (dprobs - delta)).astype(jnp.bfloat16)
        dq_ref[:, cols] = jnp.dot(dscores, k, preferred_element_type=jnp.float32)
        dk = dk + lax.dot_general(
            dscores, q, (((0,), (0,)), ((), ())), preferred_element_type=jnp.float32
        )
        dv = dv + lax.dot_general(
            probs_bf16, do, (((0,), (0,)), ((), ())), preferred_element_type=jnp.float32
        )
    dk_ref[...] = dk
    dv_ref[...] = dv


def fused_attention(q2d, k_all, v_all, do2d, lower, groups):
    rows, query_cols = q2d.shape
    keys, kv_cols = k_all.shape
    width = kv_cols // groups
    per_group = query_cols // groups
    heads = query_cols // width
    flops = 2 * rows * keys * width * 6 * heads
    io_bytes = 2 * (3 * rows * query_cols + 2 * keys * kv_cols) + 4 * (rows * query_cols + 2 * keys * kv_cols)
    return pl.pallas_call(
        attention_body,
        grid=(groups,),
        in_specs=[
            pl.BlockSpec((rows, per_group), lambda g: (0, g)),
            pl.BlockSpec((keys, width), lambda g: (0, g)),
            pl.BlockSpec((keys, width), lambda g: (0, g)),
            pl.BlockSpec((rows, per_group), lambda g: (0, g)),
            pl.BlockSpec((rows, 1), lambda g: (0, 0)),
        ],
        out_specs=[
            pl.BlockSpec((rows, per_group), lambda g: (0, g)),
            pl.BlockSpec((rows, per_group), lambda g: (0, g)),
            pl.BlockSpec((keys, width), lambda g: (0, g)),
            pl.BlockSpec((keys, width), lambda g: (0, g)),
        ],
        out_shape=[
            jax.ShapeDtypeStruct((rows, query_cols), jnp.bfloat16),
            jax.ShapeDtypeStruct((rows, query_cols), jnp.float32),
            jax.ShapeDtypeStruct((keys, kv_cols), jnp.float32),
            jax.ShapeDtypeStruct((keys, kv_cols), jnp.float32),
        ],
        compiler_params=pltpu.CompilerParams(vmem_limit_bytes=56 * 1024 * 1024),
        cost_estimate=pl.CostEstimate(
            flops=flops, transcendentals=rows * keys * heads, bytes_accessed=io_bytes
        ),
    )(q2d, k_all, v_all, do2d, lower)


def pair_term_body(mine_ref, columns_ref, theirs_ref, their_columns_ref, out_ref):
    contract = (((0,), (0,)), ((), ()))
    own = lax.dot_general(
        mine_ref[...], columns_ref[...], contract, preferred_element_type=jnp.float32
    )
    other = lax.dot_general(
        theirs_ref[...], their_columns_ref[...], contract, preferred_element_type=jnp.float32
    )
    out_ref[...] = own.astype(jnp.bfloat16).astype(jnp.float32) + other.astype(
        jnp.bfloat16
    ).astype(jnp.float32)


def pair_terms(mine, columns, theirs, their_columns):
    count, rows = mine.shape
    width = columns.shape[1]
    row_tile = math.gcd(rows, 384)
    column_tile = math.gcd(width, 512)
    row_spec = pl.BlockSpec((count, row_tile), lambda i, j: (0, i))
    column_spec = pl.BlockSpec((count, column_tile), lambda i, j: (0, j))
    return pl.pallas_call(
        pair_term_body,
        grid=(rows // row_tile, width // column_tile),
        in_specs=[row_spec, column_spec, row_spec, column_spec],
        out_specs=pl.BlockSpec((row_tile, column_tile), lambda i, j: (i, j)),
        out_shape=jax.ShapeDtypeStruct((rows, width), jnp.float32),
        cost_estimate=pl.CostEstimate(
            flops=4 * count * rows * width,
            transcendentals=0,
            bytes_accessed=4 * count * (rows + width) + 4 * rows * width,
        ),
    )(mine, columns, theirs, their_columns)


def rope_tables(positions, head_width):
    half_width = head_width // 2
    indices = jnp.arange(half_width, dtype=jnp.float32)
    frequency = jnp.power(rope_base, -2.0 * indices / head_width)
    angles = positions.astype(jnp.float32)[:, None] * frequency[None, :]
    return (jnp.cos(angles)[:, None, :], jnp.sin(angles)[:, None, :])


def rotate(vector, cosine_table, sine_table):
    half_width = vector.shape[-1] // 2
    lower_half = vector[..., :half_width]
    upper_half = vector[..., half_width:]
    return jnp.concatenate(
        [
            lower_half * cosine_table - upper_half * sine_table,
            upper_half * cosine_table + lower_half * sine_table,
        ],
        axis=-1,
    )


def unrotate(rotated, cosine_table, sine_table):
    half_width = rotated.shape[-1] // 2
    lower_half = rotated[..., :half_width]
    upper_half = rotated[..., half_width:]
    return jnp.concatenate(
        [
            lower_half * cosine_table + upper_half * sine_table,
            upper_half * cosine_table - lower_half * sine_table,
        ],
        axis=-1,
    )


def normalize(vector, gain_vector):
    inv_rms = lax.rsqrt(jnp.mean(vector * vector, axis=-1, keepdims=True) + norm_eps)
    return (vector * inv_rms * gain_vector, inv_rms)


def norm_back(vector, inv_rms, gain_vector, upstream):
    scaled = upstream * gain_vector
    return inv_rms * scaled - vector * (inv_rms * inv_rms * inv_rms) * jnp.mean(
        vector * scaled, axis=-1, keepdims=True
    )


def on_device(tokens, w_query, w_key, w_value, query_gain, key_gain, positions, out_grad):
    gathered = lax.all_gather(tokens, "head", axis=0, tiled=True)
    row_count = gathered.shape[0]
    head_width = query_gain.shape[0]
    head_count = w_query.shape[1] // head_width
    groups = w_key.shape[1] // head_width
    group_size = head_count // groups
    rank_count = lax.axis_size("ctx")
    my_rank = lax.axis_index("ctx")
    reach_blocks = min((WINDOW - 2) // row_count + 1, rank_count - 1)
    core = my_rank % CORES
    partner = [(rank, rank ^ 1) for rank in range(rank_count)]
    my_rows = pair_rows(gathered, core, rank_count)
    partner_rows = lax.ppermute(
        pair_rows(gathered, CORES - 1 - core, rank_count), "ctx", partner
    )
    query_scale = 1.0 / math.sqrt(head_width)
    query_raw = jnp.dot(gathered, w_query, preferred_element_type=jnp.float32).reshape(
        row_count, head_count, head_width
    )
    key_raw = jnp.dot(gathered, w_key, preferred_element_type=jnp.float32).reshape(
        row_count, groups, head_width
    )
    value_states = jnp.dot(gathered, w_value, preferred_element_type=jnp.float32).astype(
        jnp.bfloat16
    )
    cosine_table, sine_table = rope_tables(positions, head_width)
    query_normed, query_inv = normalize(query_raw, query_gain)
    key_normed, key_inv = normalize(key_raw, key_gain)
    query_states = (
        (rotate(query_normed, cosine_table, sine_table) * query_scale)
        .astype(jnp.bfloat16)
        .reshape(row_count, groups, group_size, head_width)
    )
    key_states = (
        rotate(key_normed, cosine_table, sine_table)
        .astype(jnp.bfloat16)
        .reshape(row_count, groups * head_width)
    )
    local_kv = jnp.stack([key_states, value_states])
    blocks = [local_kv] + [
        passed_along(local_kv, "ctx", stride) for stride in range(1, reach_blocks + 1)
    ]
    offsets = jnp.arange(row_count, dtype=jnp.int32)
    key_count = (reach_blocks + 1) * row_count
    lower = jnp.maximum(
        (reach_blocks - my_rank) * row_count,
        reach_blocks * row_count + offsets - jnp.minimum(positions, WINDOW - 1),
    )[:, None]
    ordered = blocks[::-1]
    all_keys = jnp.concatenate([block[0] for block in ordered], axis=0)
    all_values = jnp.concatenate([block[1] for block in ordered], axis=0)
    attended, query_grads, key_grad_all, value_grad_all = fused_attention(
        query_states.reshape(row_count, head_count * head_width),
        all_keys,
        all_values,
        out_grad,
        lower,
        groups,
    )

    def grad_rows(stride):
        start = key_count - (stride + 1) * row_count
        return jnp.stack(
            [
                key_grad_all[start : start + row_count],
                value_grad_all[start : start + row_count],
            ]
        )

    key_grad_parts = [grad_rows(stride) for stride in range(reach_blocks + 1)]
    returned = reduce(
        jnp.add,
        [key_grad_parts[0]]
        + [
            passed_along(key_grad_parts[stride].astype(jnp.bfloat16), "ctx", -stride).astype(
                jnp.float32
            )
            for stride in range(1, reach_blocks + 1)
        ],
    )
    key_grads = returned[0].reshape(row_count, groups, head_width)
    value_grads = returned[1].astype(jnp.bfloat16)
    query_raw_grad = (
        norm_back(
            query_raw,
            query_inv,
            query_gain,
            unrotate(
                query_grads.reshape(row_count, head_count, head_width), cosine_table, sine_table
            )
            * query_scale,
        )
        .astype(jnp.bfloat16)
        .reshape(row_count, head_count * head_width)
    )
    key_raw_grad = (
        norm_back(key_raw, key_inv, key_gain, unrotate(key_grads, cosine_table, sine_table))
        .astype(jnp.bfloat16)
        .reshape(row_count, groups * head_width)
    )
    grad_columns = jnp.concatenate([query_raw_grad, key_raw_grad, value_grads], axis=1)
    partner_columns = lax.ppermute(grad_columns, "ctx", partner)
    pair_sum = pair_terms(my_rows, grad_columns, partner_rows, partner_columns)
    pair_sum, query_raw_grad, key_raw_grad, value_grads = lax.optimization_barrier(
        (pair_sum, query_raw_grad, key_raw_grad, value_grads)
    )
    summed = torus_reduce_scatter(pair_sum, my_rank, rank_count).astype(jnp.bfloat16)
    input_terms = (
        jnp.dot(query_raw_grad, w_query.T, preferred_element_type=jnp.float32)
        + jnp.dot(key_raw_grad, w_key.T, preferred_element_type=jnp.float32)
        + jnp.dot(value_grads, w_value.T, preferred_element_type=jnp.float32)
    )
    input_grad = lax.psum_scatter(
        input_terms.astype(jnp.bfloat16), "head", scatter_dimension=0, tiled=True
    )
    query_cols = head_count * head_width
    key_cols = groups * head_width
    return (
        attended.reshape(row_count, query_cols),
        input_grad,
        summed[:, :query_cols],
        summed[:, query_cols : query_cols + key_cols],
        summed[:, query_cols + key_cols :],
    )


def solution(mesh):
    in_specs = (
        P(("ctx", "head"), None),
        P(None, "head"),
        P(None, "head"),
        P(None, "head"),
        P(),
        P(),
        P("ctx"),
        P("ctx", "head"),
    )
    out_specs = (
        P("ctx", "head"),
        P(("ctx", "head"), None),
        P("ctx", "head"),
        P("ctx", "head"),
        P("ctx", "head"),
    )
    return jax.shard_map(
        on_device, mesh=mesh, in_specs=in_specs, out_specs=out_specs, check_vma=False
    )
```

```python
from functools import reduce
import math

import jax
import jax.numpy as jnp
from jax import lax
from jax.experimental import pallas as pl
from jax.experimental.pallas import tpu as pltpu
from jax.sharding import PartitionSpec as P

WINDOW = 1024


norm_eps = 1e-06
rope_base = 10000.0


def passed_along(block, axis, distance):
    devices = range(lax.axis_size(axis))
    route = [(i - distance, i) for i in devices if i - distance in devices]
    return lax.ppermute(block, axis, route)


CORES = 2
Y_CHIPS = 4


def ring_pairs(rank_count, along_y):
    z_chips = rank_count // (CORES * Y_CHIPS)
    forward = []
    for z in range(z_chips):
        for y in range(Y_CHIPS):
            for core in range(CORES):
                source = (z * Y_CHIPS + y) * CORES + core
                if along_y:
                    target = (z * Y_CHIPS + (y + 1) % Y_CHIPS) * CORES + core
                else:
                    target = (((z + 1) % z_chips) * Y_CHIPS + y) * CORES + core
                forward.append((source, target))
    backward = [(target, source) for source, target in forward]
    return forward, backward


def ring_reduce_scatter(parts, axis, position, forward, backward):
    count = parts.shape[axis]
    half = parts.shape[-1] // 2

    def own(index, low):
        piece = lax.slice_in_dim(parts, low, low + half, axis=parts.ndim - 1)
        return lax.dynamic_index_in_dim(piece, index % count, axis, keepdims=False)

    up = own(position + count - 1, 0)
    down = own(position + 1, half)
    for step in range(count - 1):
        up = lax.ppermute(up.astype(jnp.bfloat16), "ctx", forward).astype(jnp.float32) + own(
            position + 2 * count - step - 2, 0
        )
        down = lax.ppermute(down.astype(jnp.bfloat16), "ctx", backward).astype(
            jnp.float32
        ) + own(position + step + 2, half)
    return jnp.concatenate([up, down], axis=-1)


def pair_rows(gathered, core, rank_count):
    z_chips = rank_count // (CORES * Y_CHIPS)
    count, width = gathered.shape
    grid = gathered.reshape(count, z_chips, Y_CHIPS, CORES, width // rank_count)
    return lax.dynamic_index_in_dim(grid, core, 3, keepdims=False).reshape(count, width // CORES)


def rounded_term(rows, columns):
    return (
        lax.dot_general(rows, columns, (((0,), (0,)), ((), ())), preferred_element_type=jnp.float32)
        .astype(jnp.bfloat16)
        .astype(jnp.float32)
    )


def torus_reduce_scatter(first, second, my_rank, rank_count):
    z_chips = rank_count // (CORES * Y_CHIPS)
    rows = first.shape[0]
    y_pos = (my_rank // CORES) % Y_CHIPS
    z_pos = my_rank // (CORES * Y_CHIPS)
    per_rank = rows // (z_chips * Y_CHIPS)
    first = first.reshape(z_chips, Y_CHIPS, per_rank, first.shape[-1])
    second = second.reshape(z_chips, Y_CHIPS, per_rank, second.shape[-1])
    y_forward, y_backward = ring_pairs(rank_count, True)
    z_forward, z_backward = ring_pairs(rank_count, False)
    first = ring_reduce_scatter(first, 1, y_pos, y_forward, y_backward)
    first = ring_reduce_scatter(first, 0, z_pos, z_forward, z_backward)
    second = ring_reduce_scatter(second, 0, z_pos, z_forward, z_backward)
    second = ring_reduce_scatter(second, 0, y_pos, y_forward, y_backward)
    return jnp.concatenate([first, second], axis=-1)


def attention_body(q_ref, k_ref, v_ref, do_ref, lo_ref, att_ref, dq_ref, dk_ref, dv_ref):
    rows = q_ref.shape[0]
    keys, width = k_ref.shape
    k = k_ref[...]
    v = v_ref[...]
    key_index = lax.broadcasted_iota(jnp.int32, (rows, keys), 1)
    query_index = lax.broadcasted_iota(jnp.int32, (rows, keys), 0)
    visible = (key_index >= lo_ref[...]) & (key_index <= query_index + (keys - rows))
    dk = jnp.zeros((keys, width), jnp.float32)
    dv = jnp.zeros((keys, width), jnp.float32)
    for head in range(q_ref.shape[1] // width):
        cols = slice(head * width, (head + 1) * width)
        q = q_ref[:, cols]
        do = do_ref[:, cols]
        scores = lax.dot_general(q, k, (((1,), (1,)), ((), ())), preferred_element_type=jnp.float32)
        peak = jnp.max(jnp.where(visible, scores, -jnp.inf), axis=-1, keepdims=True)
        weights = jnp.where(visible, jnp.exp(scores - peak), 0.0)
        probs = weights / jnp.sum(weights, axis=-1, keepdims=True)
        probs_bf16 = probs.astype(jnp.bfloat16)
        attended = jnp.dot(probs_bf16, v, preferred_element_type=jnp.float32).astype(jnp.bfloat16)
        att_ref[:, cols] = attended
        delta = jnp.sum(
            do.astype(jnp.float32) * attended.astype(jnp.float32), axis=-1, keepdims=True
        )
        dprobs = lax.dot_general(do, v, (((1,), (1,)), ((), ())), preferred_element_type=jnp.float32)
        dscores = (probs * (dprobs - delta)).astype(jnp.bfloat16)
        dq_ref[:, cols] = jnp.dot(dscores, k, preferred_element_type=jnp.float32)
        dk = dk + lax.dot_general(
            dscores, q, (((0,), (0,)), ((), ())), preferred_element_type=jnp.float32
        )
        dv = dv + lax.dot_general(
            probs_bf16, do, (((0,), (0,)), ((), ())), preferred_element_type=jnp.float32
        )
    dk_ref[...] = dk
    dv_ref[...] = dv


def fused_attention(q2d, k_all, v_all, do2d, lower, groups):
    rows, query_cols = q2d.shape
    keys, kv_cols = k_all.shape
    width = kv_cols // groups
    per_group = query_cols // groups
    heads = query_cols // width
    flops = 2 * rows * keys * width * 6 * heads
    io_bytes = 2 * (3 * rows * query_cols + 2 * keys * kv_cols) + 4 * (rows * query_cols + 2 * keys * kv_cols)
    return pl.pallas_call(
        attention_body,
        grid=(groups,),
        in_specs=[
            pl.BlockSpec((rows, per_group), lambda g: (0, g)),
            pl.BlockSpec((keys, width), lambda g: (0, g)),
            pl.BlockSpec((keys, width), lambda g: (0, g)),
            pl.BlockSpec((rows, per_group), lambda g: (0, g)),
            pl.BlockSpec((rows, 1), lambda g: (0, 0)),
        ],
        out_specs=[
            pl.BlockSpec((rows, per_group), lambda g: (0, g)),
            pl.BlockSpec((rows, per_group), lambda g: (0, g)),
            pl.BlockSpec((keys, width), lambda g: (0, g)),
            pl.BlockSpec((keys, width), lambda g: (0, g)),
        ],
        out_shape=[
            jax.ShapeDtypeStruct((rows, query_cols), jnp.bfloat16),
            jax.ShapeDtypeStruct((rows, query_cols), jnp.float32),
            jax.ShapeDtypeStruct((keys, kv_cols), jnp.float32),
            jax.ShapeDtypeStruct((keys, kv_cols), jnp.float32),
        ],
        compiler_params=pltpu.CompilerParams(vmem_limit_bytes=56 * 1024 * 1024),
        cost_estimate=pl.CostEstimate(
            flops=flops, transcendentals=rows * keys * heads, bytes_accessed=io_bytes
        ),
    )(q2d, k_all, v_all, do2d, lower)


def rope_tables(positions, head_width):
    half_width = head_width // 2
    indices = jnp.arange(half_width, dtype=jnp.float32)
    frequency = jnp.power(rope_base, -2.0 * indices / head_width)
    angles = positions.astype(jnp.float32)[:, None] * frequency[None, :]
    return (jnp.cos(angles)[:, None, :], jnp.sin(angles)[:, None, :])


def rotate(vector, cosine_table, sine_table):
    half_width = vector.shape[-1] // 2
    lower_half = vector[..., :half_width]
    upper_half = vector[..., half_width:]
    return jnp.concatenate(
        [
            lower_half * cosine_table - upper_half * sine_table,
            upper_half * cosine_table + lower_half * sine_table,
        ],
        axis=-1,
    )


def unrotate(rotated, cosine_table, sine_table):
    half_width = rotated.shape[-1] // 2
    lower_half = rotated[..., :half_width]
    upper_half = rotated[..., half_width:]
    return jnp.concatenate(
        [
            lower_half * cosine_table + upper_half * sine_table,
            upper_half * cosine_table - lower_half * sine_table,
        ],
        axis=-1,
    )


def normalize(vector, gain_vector):
    inv_rms = lax.rsqrt(jnp.mean(vector * vector, axis=-1, keepdims=True) + norm_eps)
    return (vector * inv_rms * gain_vector, inv_rms)


def norm_back(vector, inv_rms, gain_vector, upstream):
    scaled = upstream * gain_vector
    return inv_rms * scaled - vector * (inv_rms * inv_rms * inv_rms) * jnp.mean(
        vector * scaled, axis=-1, keepdims=True
    )


def on_device(tokens, w_query, w_key, w_value, query_gain, key_gain, positions, out_grad):
    gathered = lax.all_gather(tokens, "head", axis=0, tiled=True)
    row_count = gathered.shape[0]
    head_width = query_gain.shape[0]
    head_count = w_query.shape[1] // head_width
    groups = w_key.shape[1] // head_width
    group_size = head_count // groups
    rank_count = lax.axis_size("ctx")
    my_rank = lax.axis_index("ctx")
    reach_blocks = min((WINDOW - 2) // row_count + 1, rank_count - 1)
    core = my_rank % CORES
    partner = [(rank, rank ^ 1) for rank in range(rank_count)]
    my_rows = pair_rows(gathered, core, rank_count)
    partner_rows = lax.ppermute(
        pair_rows(gathered, CORES - 1 - core, rank_count), "ctx", partner
    )
    query_scale = 1.0 / math.sqrt(head_width)
    query_raw = jnp.dot(gathered, w_query, preferred_element_type=jnp.float32).reshape(
        row_count, head_count, head_width
    )
    key_raw = jnp.dot(gathered, w_key, preferred_element_type=jnp.float32).reshape(
        row_count, groups, head_width
    )
    value_states = jnp.dot(gathered, w_value, preferred_element_type=jnp.float32).astype(
        jnp.bfloat16
    )
    cosine_table, sine_table = rope_tables(positions, head_width)
    query_normed, query_inv = normalize(query_raw, query_gain)
    key_normed, key_inv = normalize(key_raw, key_gain)
    query_states = (
        (rotate(query_normed, cosine_table, sine_table) * query_scale)
        .astype(jnp.bfloat16)
        .reshape(row_count, groups, group_size, head_width)
    )
    key_states = (
        rotate(key_normed, cosine_table, sine_table)
        .astype(jnp.bfloat16)
        .reshape(row_count, groups * head_width)
    )
    local_kv = jnp.stack([key_states, value_states])
    blocks = [local_kv] + [
        passed_along(local_kv, "ctx", stride) for stride in range(1, reach_blocks + 1)
    ]
    offsets = jnp.arange(row_count, dtype=jnp.int32)
    key_count = (reach_blocks + 1) * row_count
    lower = jnp.maximum(
        (reach_blocks - my_rank) * row_count,
        reach_blocks * row_count + offsets - jnp.minimum(positions, WINDOW - 1),
    )[:, None]
    ordered = blocks[::-1]
    all_keys = jnp.concatenate([block[0] for block in ordered], axis=0)
    all_values = jnp.concatenate([block[1] for block in ordered], axis=0)
    attended, query_grads, key_grad_all, value_grad_all = fused_attention(
        query_states.reshape(row_count, head_count * head_width),
        all_keys,
        all_values,
        out_grad,
        lower,
        groups,
    )

    def grad_rows(stride):
        start = key_count - (stride + 1) * row_count
        return jnp.stack(
            [
                key_grad_all[start : start + row_count],
                value_grad_all[start : start + row_count],
            ]
        )

    key_grad_parts = [grad_rows(stride) for stride in range(reach_blocks + 1)]
    returned = reduce(
        jnp.add,
        [key_grad_parts[0]]
        + [
            passed_along(key_grad_parts[stride].astype(jnp.bfloat16), "ctx", -stride).astype(
                jnp.float32
            )
            for stride in range(1, reach_blocks + 1)
        ],
    )
    key_grads = returned[0].reshape(row_count, groups, head_width)
    value_grads = returned[1].astype(jnp.bfloat16)
    query_raw_grad = (
        norm_back(
            query_raw,
            query_inv,
            query_gain,
            unrotate(
                query_grads.reshape(row_count, head_count, head_width), cosine_table, sine_table
            )
            * query_scale,
        )
        .astype(jnp.bfloat16)
        .reshape(row_count, head_count * head_width)
    )
    key_raw_grad = (
        norm_back(key_raw, key_inv, key_gain, unrotate(key_grads, cosine_table, sine_table))
        .astype(jnp.bfloat16)
        .reshape(row_count, groups * head_width)
    )
    query_sum = rounded_term(my_rows, query_raw_grad) + rounded_term(
        partner_rows, lax.ppermute(query_raw_grad, "ctx", partner)
    )
    kv_columns = jnp.concatenate([key_raw_grad, value_grads], axis=1)
    kv_sum = rounded_term(my_rows, kv_columns) + rounded_term(
        partner_rows, lax.ppermute(kv_columns, "ctx", partner)
    )
    kv_sum, query_raw_grad, key_raw_grad, value_grads = lax.optimization_barrier(
        (kv_sum, query_raw_grad, key_raw_grad, value_grads)
    )
    summed = torus_reduce_scatter(query_sum, kv_sum, my_rank, rank_count).astype(
        jnp.bfloat16
    )
    input_terms = (
        jnp.dot(query_raw_grad, w_query.T, preferred_element_type=jnp.float32)
        + jnp.dot(key_raw_grad, w_key.T, preferred_element_type=jnp.float32)
        + jnp.dot(value_grads, w_value.T, preferred_element_type=jnp.float32)
    )
    input_grad = lax.psum_scatter(
        input_terms.astype(jnp.bfloat16), "head", scatter_dimension=0, tiled=True
    )
    query_cols = head_count * head_width
    key_cols = groups * head_width
    return (
        attended.reshape(row_count, query_cols),
        input_grad,
        summed[:, :query_cols],
        summed[:, query_cols : query_cols + key_cols],
        summed[:, query_cols + key_cols :],
    )


def solution(mesh):
    in_specs = (
        P(("ctx", "head"), None),
        P(None, "head"),
        P(None, "head"),
        P(None, "head"),
        P(),
        P(),
        P("ctx"),
        P("ctx", "head"),
    )
    out_specs = (
        P("ctx", "head"),
        P(("ctx", "head"), None),
        P("ctx", "head"),
        P("ctx", "head"),
        P("ctx", "head"),
    )
    return jax.shard_map(
        on_device, mesh=mesh, in_specs=in_specs, out_specs=out_specs, check_vma=False
    )
```

```python
from functools import reduce
import math

import jax
import jax.numpy as jnp
from jax import lax
from jax.experimental import pallas as pl
from jax.experimental.pallas import tpu as pltpu
from jax.sharding import PartitionSpec as P

WINDOW = 1024


norm_eps = 1e-06
rope_base = 10000.0


def passed_along(block, axis, distance):
    devices = range(lax.axis_size(axis))
    route = [(i - distance, i) for i in devices if i - distance in devices]
    return lax.ppermute(block, axis, route)


CORES = 2
Y_CHIPS = 4


def ring_pairs(rank_count, along_y):
    z_chips = rank_count // (CORES * Y_CHIPS)
    forward = []
    for z in range(z_chips):
        for y in range(Y_CHIPS):
            for core in range(CORES):
                source = (z * Y_CHIPS + y) * CORES + core
                if along_y:
                    target = (z * Y_CHIPS + (y + 1) % Y_CHIPS) * CORES + core
                else:
                    target = (((z + 1) % z_chips) * Y_CHIPS + y) * CORES + core
                forward.append((source, target))
    backward = [(target, source) for source, target in forward]
    return forward, backward


def ring_reduce_scatter(parts, axis, position, forward, backward):
    count = parts.shape[axis]
    half = parts.shape[-1] // 2

    def own(index, low):
        piece = lax.slice_in_dim(parts, low, low + half, axis=parts.ndim - 1)
        return lax.dynamic_index_in_dim(piece, index % count, axis, keepdims=False).astype(
            jnp.float32
        )

    up = own(position + count - 1, 0)
    down = own(position + 1, half)
    for step in range(count - 1):
        up = lax.ppermute(up.astype(jnp.bfloat16), "ctx", forward).astype(jnp.float32) + own(
            position + 2 * count - step - 2, 0
        )
        down = lax.ppermute(down.astype(jnp.bfloat16), "ctx", backward).astype(
            jnp.float32
        ) + own(position + step + 2, half)
    return jnp.concatenate([up, down], axis=-1)


def pair_rows(gathered, core, rank_count):
    z_chips = rank_count // (CORES * Y_CHIPS)
    count, width = gathered.shape
    grid = gathered.reshape(count, z_chips, Y_CHIPS, CORES, width // rank_count)
    return lax.dynamic_index_in_dim(grid, core, 3, keepdims=False).reshape(count, width // CORES)


def rounded_term(rows, columns):
    return (
        lax.dot_general(rows, columns, (((0,), (0,)), ((), ())), preferred_element_type=jnp.float32)
        .astype(jnp.bfloat16)
        .astype(jnp.float32)
    )


def torus_reduce_scatter(pair_sum, my_rank, rank_count):
    z_chips = rank_count // (CORES * Y_CHIPS)
    rows, columns = pair_sum.shape
    y_pos = (my_rank // CORES) % Y_CHIPS
    z_pos = my_rank // (CORES * Y_CHIPS)
    grid = pair_sum.reshape(z_chips, Y_CHIPS, rows // (z_chips * Y_CHIPS), columns)
    y_forward, y_backward = ring_pairs(rank_count, True)
    z_forward, z_backward = ring_pairs(rank_count, False)
    half = columns // 2
    first = grid[..., :half]
    second = grid[..., half:]
    first = ring_reduce_scatter(first, 1, y_pos, y_forward, y_backward)
    first = ring_reduce_scatter(first, 0, z_pos, z_forward, z_backward)
    second = ring_reduce_scatter(second, 0, z_pos, z_forward, z_backward)
    second = ring_reduce_scatter(second, 0, y_pos, y_forward, y_backward)
    return jnp.concatenate([first, second], axis=-1)


def attention_body(q_ref, k_ref, v_ref, do_ref, lo_ref, att_ref, dq_ref, dk_ref, dv_ref):
    rows = q_ref.shape[0]
    keys, width = k_ref.shape
    k = k_ref[...]
    v = v_ref[...]
    key_index = lax.broadcasted_iota(jnp.int32, (rows, keys), 1)
    query_index = lax.broadcasted_iota(jnp.int32, (rows, keys), 0)
    visible = (key_index >= lo_ref[...]) & (key_index <= query_index + (keys - rows))
    dk = jnp.zeros((keys, width), jnp.float32)
    dv = jnp.zeros((keys, width), jnp.float32)
    for head in range(q_ref.shape[1] // width):
        cols = slice(head * width, (head + 1) * width)
        q = q_ref[:, cols]
        do = do_ref[:, cols]
        scores = lax.dot_general(q, k, (((1,), (1,)), ((), ())), preferred_element_type=jnp.float32)
        peak = jnp.max(jnp.where(visible, scores, -jnp.inf), axis=-1, keepdims=True)
        weights = jnp.where(visible, jnp.exp(scores - peak), 0.0)
        probs = weights / jnp.sum(weights, axis=-1, keepdims=True)
        probs_bf16 = probs.astype(jnp.bfloat16)
        attended = jnp.dot(probs_bf16, v, preferred_element_type=jnp.float32).astype(jnp.bfloat16)
        att_ref[:, cols] = attended
        delta = jnp.sum(
            do.astype(jnp.float32) * attended.astype(jnp.float32), axis=-1, keepdims=True
        )
        dprobs = lax.dot_general(do, v, (((1,), (1,)), ((), ())), preferred_element_type=jnp.float32)
        dscores = (probs * (dprobs - delta)).astype(jnp.bfloat16)
        dq_ref[:, cols] = jnp.dot(dscores, k, preferred_element_type=jnp.float32)
        dk = dk + lax.dot_general(
            dscores, q, (((0,), (0,)), ((), ())), preferred_element_type=jnp.float32
        )
        dv = dv + lax.dot_general(
            probs_bf16, do, (((0,), (0,)), ((), ())), preferred_element_type=jnp.float32
        )
    dk_ref[...] = dk
    dv_ref[...] = dv


def fused_attention(q2d, k_all, v_all, do2d, lower, groups):
    rows, query_cols = q2d.shape
    keys, kv_cols = k_all.shape
    width = kv_cols // groups
    per_group = query_cols // groups
    heads = query_cols // width
    flops = 2 * rows * keys * width * 6 * heads
    io_bytes = 2 * (3 * rows * query_cols + 2 * keys * kv_cols) + 4 * (rows * query_cols + 2 * keys * kv_cols)
    return pl.pallas_call(
        attention_body,
        grid=(groups,),
        in_specs=[
            pl.BlockSpec((rows, per_group), lambda g: (0, g)),
            pl.BlockSpec((keys, width), lambda g: (0, g)),
            pl.BlockSpec((keys, width), lambda g: (0, g)),
            pl.BlockSpec((rows, per_group), lambda g: (0, g)),
            pl.BlockSpec((rows, 1), lambda g: (0, 0)),
        ],
        out_specs=[
            pl.BlockSpec((rows, per_group), lambda g: (0, g)),
            pl.BlockSpec((rows, per_group), lambda g: (0, g)),
            pl.BlockSpec((keys, width), lambda g: (0, g)),
            pl.BlockSpec((keys, width), lambda g: (0, g)),
        ],
        out_shape=[
            jax.ShapeDtypeStruct((rows, query_cols), jnp.bfloat16),
            jax.ShapeDtypeStruct((rows, query_cols), jnp.float32),
            jax.ShapeDtypeStruct((keys, kv_cols), jnp.float32),
            jax.ShapeDtypeStruct((keys, kv_cols), jnp.float32),
        ],
        compiler_params=pltpu.CompilerParams(vmem_limit_bytes=56 * 1024 * 1024),
        cost_estimate=pl.CostEstimate(
            flops=flops, transcendentals=rows * keys * heads, bytes_accessed=io_bytes
        ),
    )(q2d, k_all, v_all, do2d, lower)


def rope_tables(positions, head_width):
    half_width = head_width // 2
    indices = jnp.arange(half_width, dtype=jnp.float32)
    frequency = jnp.power(rope_base, -2.0 * indices / head_width)
    angles = positions.astype(jnp.float32)[:, None] * frequency[None, :]
    return (jnp.cos(angles)[:, None, :], jnp.sin(angles)[:, None, :])


def rotate(vector, cosine_table, sine_table):
    half_width = vector.shape[-1] // 2
    lower_half = vector[..., :half_width]
    upper_half = vector[..., half_width:]
    return jnp.concatenate(
        [
            lower_half * cosine_table - upper_half * sine_table,
            upper_half * cosine_table + lower_half * sine_table,
        ],
        axis=-1,
    )


def unrotate(rotated, cosine_table, sine_table):
    half_width = rotated.shape[-1] // 2
    lower_half = rotated[..., :half_width]
    upper_half = rotated[..., half_width:]
    return jnp.concatenate(
        [
            lower_half * cosine_table + upper_half * sine_table,
            upper_half * cosine_table - lower_half * sine_table,
        ],
        axis=-1,
    )


def normalize(vector, gain_vector):
    inv_rms = lax.rsqrt(jnp.mean(vector * vector, axis=-1, keepdims=True) + norm_eps)
    return (vector * inv_rms * gain_vector, inv_rms)


def norm_back(vector, inv_rms, gain_vector, upstream):
    scaled = upstream * gain_vector
    return inv_rms * scaled - vector * (inv_rms * inv_rms * inv_rms) * jnp.mean(
        vector * scaled, axis=-1, keepdims=True
    )


def on_device(tokens, w_query, w_key, w_value, query_gain, key_gain, positions, out_grad):
    gathered = lax.all_gather(tokens, "head", axis=0, tiled=True)
    row_count = gathered.shape[0]
    head_width = query_gain.shape[0]
    head_count = w_query.shape[1] // head_width
    groups = w_key.shape[1] // head_width
    group_size = head_count // groups
    rank_count = lax.axis_size("ctx")
    my_rank = lax.axis_index("ctx")
    reach_blocks = min((WINDOW - 2) // row_count + 1, rank_count - 1)
    core = my_rank % CORES
    partner = [(rank, rank ^ 1) for rank in range(rank_count)]
    my_rows = pair_rows(gathered, core, rank_count)
    partner_rows = lax.ppermute(
        pair_rows(gathered, CORES - 1 - core, rank_count), "ctx", partner
    )
    query_scale = 1.0 / math.sqrt(head_width)
    query_raw = jnp.dot(gathered, w_query, preferred_element_type=jnp.float32).reshape(
        row_count, head_count, head_width
    )
    key_raw = jnp.dot(gathered, w_key, preferred_element_type=jnp.float32).reshape(
        row_count, groups, head_width
    )
    value_states = jnp.dot(gathered, w_value, preferred_element_type=jnp.float32).astype(
        jnp.bfloat16
    )
    cosine_table, sine_table = rope_tables(positions, head_width)
    query_normed, query_inv = normalize(query_raw, query_gain)
    key_normed, key_inv = normalize(key_raw, key_gain)
    query_states = (
        (rotate(query_normed, cosine_table, sine_table) * query_scale)
        .astype(jnp.bfloat16)
        .reshape(row_count, groups, group_size, head_width)
    )
    key_states = (
        rotate(key_normed, cosine_table, sine_table)
        .astype(jnp.bfloat16)
        .reshape(row_count, groups * head_width)
    )
    local_kv = jnp.stack([key_states, value_states])
    blocks = [local_kv] + [
        passed_along(local_kv, "ctx", stride) for stride in range(1, reach_blocks + 1)
    ]
    offsets = jnp.arange(row_count, dtype=jnp.int32)
    key_count = (reach_blocks + 1) * row_count
    lower = jnp.maximum(
        (reach_blocks - my_rank) * row_count,
        reach_blocks * row_count + offsets - jnp.minimum(positions, WINDOW - 1),
    )[:, None]
    ordered = blocks[::-1]
    all_keys = jnp.concatenate([block[0] for block in ordered], axis=0)
    all_values = jnp.concatenate([block[1] for block in ordered], axis=0)
    attended, query_grads, key_grad_all, value_grad_all = fused_attention(
        query_states.reshape(row_count, head_count * head_width),
        all_keys,
        all_values,
        out_grad,
        lower,
        groups,
    )

    def grad_rows(stride):
        start = key_count - (stride + 1) * row_count
        return jnp.stack(
            [
                key_grad_all[start : start + row_count],
                value_grad_all[start : start + row_count],
            ]
        )

    key_grad_parts = [grad_rows(stride) for stride in range(reach_blocks + 1)]
    returned = reduce(
        jnp.add,
        [key_grad_parts[0]]
        + [
            passed_along(key_grad_parts[stride].astype(jnp.bfloat16), "ctx", -stride).astype(
                jnp.float32
            )
            for stride in range(1, reach_blocks + 1)
        ],
    )
    key_grads = returned[0].reshape(row_count, groups, head_width)
    value_grads = returned[1].astype(jnp.bfloat16)
    query_raw_grad = (
        norm_back(
            query_raw,
            query_inv,
            query_gain,
            unrotate(
                query_grads.reshape(row_count, head_count, head_width), cosine_table, sine_table
            )
            * query_scale,
        )
        .astype(jnp.bfloat16)
        .reshape(row_count, head_count * head_width)
    )
    key_raw_grad = (
        norm_back(key_raw, key_inv, key_gain, unrotate(key_grads, cosine_table, sine_table))
        .astype(jnp.bfloat16)
        .reshape(row_count, groups * head_width)
    )
    grad_columns = jnp.concatenate([query_raw_grad, key_raw_grad, value_grads], axis=1)
    partner_columns = lax.ppermute(grad_columns, "ctx", partner)
    pair_sum = (
        rounded_term(my_rows, grad_columns) + rounded_term(partner_rows, partner_columns)
    ).astype(jnp.bfloat16)
    pair_sum, query_raw_grad, key_raw_grad, value_grads = lax.optimization_barrier(
        (pair_sum, query_raw_grad, key_raw_grad, value_grads)
    )
    summed = torus_reduce_scatter(pair_sum, my_rank, rank_count).astype(jnp.bfloat16)
    input_terms = (
        jnp.dot(query_raw_grad, w_query.T, preferred_element_type=jnp.float32)
        + jnp.dot(key_raw_grad, w_key.T, preferred_element_type=jnp.float32)
        + jnp.dot(value_grads, w_value.T, preferred_element_type=jnp.float32)
    )
    input_grad = lax.psum_scatter(
        input_terms.astype(jnp.bfloat16), "head", scatter_dimension=0, tiled=True
    )
    query_cols = head_count * head_width
    key_cols = groups * head_width
    return (
        attended.reshape(row_count, query_cols),
        input_grad,
        summed[:, :query_cols],
        summed[:, query_cols : query_cols + key_cols],
        summed[:, query_cols + key_cols :],
    )


def solution(mesh):
    in_specs = (
        P(("ctx", "head"), None),
        P(None, "head"),
        P(None, "head"),
        P(None, "head"),
        P(),
        P(),
        P("ctx"),
        P("ctx", "head"),
    )
    out_specs = (
        P("ctx", "head"),
        P(("ctx", "head"), None),
        P("ctx", "head"),
        P("ctx", "head"),
        P("ctx", "head"),
    )
    return jax.shard_map(
        on_device, mesh=mesh, in_specs=in_specs, out_specs=out_specs, check_vma=False
    )
```

```python
from functools import reduce
import math

import jax
import jax.numpy as jnp
from jax import lax
from jax.experimental import pallas as pl
from jax.experimental.pallas import tpu as pltpu
from jax.sharding import PartitionSpec as P

WINDOW = 1024


norm_eps = 1e-06
rope_base = 10000.0


def passed_along(block, axis, distance):
    devices = range(lax.axis_size(axis))
    route = [(i - distance, i) for i in devices if i - distance in devices]
    return lax.ppermute(block, axis, route)


CORES = 2
Y_CHIPS = 4


def ring_pairs(rank_count, along_y):
    z_chips = rank_count // (CORES * Y_CHIPS)
    forward = []
    for z in range(z_chips):
        for y in range(Y_CHIPS):
            for core in range(CORES):
                source = (z * Y_CHIPS + y) * CORES + core
                if along_y:
                    target = (z * Y_CHIPS + (y + 1) % Y_CHIPS) * CORES + core
                else:
                    target = (((z + 1) % z_chips) * Y_CHIPS + y) * CORES + core
                forward.append((source, target))
    backward = [(target, source) for source, target in forward]
    return forward, backward


def ring_reduce_scatter(parts, axis, position, forward, backward):
    count = parts.shape[axis]
    half = parts.shape[-1] // 2

    def own(index, low):
        piece = lax.slice_in_dim(parts, low, low + half, axis=parts.ndim - 1)
        return lax.dynamic_index_in_dim(piece, index % count, axis, keepdims=False).astype(
            jnp.float32
        )

    up = own(position + count - 1, 0)
    down = own(position + 1, half)
    for step in range(count - 1):
        up = lax.ppermute(up.astype(jnp.bfloat16), "ctx", forward).astype(jnp.float32) + own(
            position + 2 * count - step - 2, 0
        )
        down = lax.ppermute(down.astype(jnp.bfloat16), "ctx", backward).astype(
            jnp.float32
        ) + own(position + step + 2, half)
    return jnp.concatenate([up, down], axis=-1)


def pair_rows(gathered, core, rank_count):
    z_chips = rank_count // (CORES * Y_CHIPS)
    count, width = gathered.shape
    grid = gathered.reshape(count, z_chips, Y_CHIPS, CORES, width // rank_count)
    return lax.dynamic_index_in_dim(grid, core, 3, keepdims=False).reshape(count, width // CORES)


def rounded_term(rows, columns):
    return (
        lax.dot_general(rows, columns, (((0,), (0,)), ((), ())), preferred_element_type=jnp.float32)
        .astype(jnp.bfloat16)
        .astype(jnp.float32)
    )


def torus_reduce_scatter(pair_sum, my_rank, rank_count):
    z_chips = rank_count // (CORES * Y_CHIPS)
    rows, columns = pair_sum.shape
    y_pos = (my_rank // CORES) % Y_CHIPS
    z_pos = my_rank // (CORES * Y_CHIPS)
    grid = pair_sum.reshape(z_chips, Y_CHIPS, rows // (z_chips * Y_CHIPS), columns)
    y_forward, y_backward = ring_pairs(rank_count, True)
    z_forward, z_backward = ring_pairs(rank_count, False)
    half = columns // 2
    first = grid[..., :half]
    second = grid[..., half:]
    first = ring_reduce_scatter(first, 1, y_pos, y_forward, y_backward)
    first = ring_reduce_scatter(first, 0, z_pos, z_forward, z_backward)
    second = ring_reduce_scatter(second, 0, z_pos, z_forward, z_backward)
    second = ring_reduce_scatter(second, 0, y_pos, y_forward, y_backward)
    return jnp.concatenate([first, second], axis=-1)


def attention_body(q_ref, k_ref, v_ref, do_ref, lo_ref, att_ref, dq_ref, dk_ref, dv_ref):
    rows = q_ref.shape[0]
    keys, width = k_ref.shape
    k = k_ref[...]
    v = v_ref[...]
    key_index = lax.broadcasted_iota(jnp.int32, (rows, keys), 1)
    query_index = lax.broadcasted_iota(jnp.int32, (rows, keys), 0)
    visible = (key_index >= lo_ref[...]) & (key_index <= query_index + (keys - rows))
    dk = jnp.zeros((keys, width), jnp.float32)
    dv = jnp.zeros((keys, width), jnp.float32)
    for head in range(q_ref.shape[1] // width):
        cols = slice(head * width, (head + 1) * width)
        q = q_ref[:, cols]
        do = do_ref[:, cols]
        scores = lax.dot_general(q, k, (((1,), (1,)), ((), ())), preferred_element_type=jnp.float32)
        peak = jnp.max(jnp.where(visible, scores, -jnp.inf), axis=-1, keepdims=True)
        weights = jnp.where(visible, jnp.exp(scores - peak), 0.0)
        probs = weights / jnp.sum(weights, axis=-1, keepdims=True)
        probs_bf16 = probs.astype(jnp.bfloat16)
        attended = jnp.dot(probs_bf16, v, preferred_element_type=jnp.float32).astype(jnp.bfloat16)
        att_ref[:, cols] = attended
        delta = jnp.sum(
            do.astype(jnp.float32) * attended.astype(jnp.float32), axis=-1, keepdims=True
        )
        dprobs = lax.dot_general(do, v, (((1,), (1,)), ((), ())), preferred_element_type=jnp.float32)
        dscores = (probs * (dprobs - delta)).astype(jnp.bfloat16)
        dq_ref[:, cols] = jnp.dot(dscores, k, preferred_element_type=jnp.float32)
        dk = dk + lax.dot_general(
            dscores, q, (((0,), (0,)), ((), ())), preferred_element_type=jnp.float32
        )
        dv = dv + lax.dot_general(
            probs_bf16, do, (((0,), (0,)), ((), ())), preferred_element_type=jnp.float32
        )
    dk_ref[...] = dk.astype(dk_ref.dtype)
    dv_ref[...] = dv.astype(dv_ref.dtype)


def fused_attention(q2d, k_all, v_all, do2d, lower, groups):
    rows, query_cols = q2d.shape
    keys, kv_cols = k_all.shape
    width = kv_cols // groups
    per_group = query_cols // groups
    heads = query_cols // width
    flops = 2 * rows * keys * width * 6 * heads
    io_bytes = 2 * (3 * rows * query_cols + 2 * keys * kv_cols) + 4 * (rows * query_cols + 2 * keys * kv_cols)
    return pl.pallas_call(
        attention_body,
        grid=(groups,),
        in_specs=[
            pl.BlockSpec((rows, per_group), lambda g: (0, g)),
            pl.BlockSpec((keys, width), lambda g: (0, g)),
            pl.BlockSpec((keys, width), lambda g: (0, g)),
            pl.BlockSpec((rows, per_group), lambda g: (0, g)),
            pl.BlockSpec((rows, 1), lambda g: (0, 0)),
        ],
        out_specs=[
            pl.BlockSpec((rows, per_group), lambda g: (0, g)),
            pl.BlockSpec((rows, per_group), lambda g: (0, g)),
            pl.BlockSpec((keys, width), lambda g: (0, g)),
            pl.BlockSpec((keys, width), lambda g: (0, g)),
        ],
        out_shape=[
            jax.ShapeDtypeStruct((rows, query_cols), jnp.bfloat16),
            jax.ShapeDtypeStruct((rows, query_cols), jnp.float32),
            jax.ShapeDtypeStruct((keys, kv_cols), jnp.bfloat16),
            jax.ShapeDtypeStruct((keys, kv_cols), jnp.bfloat16),
        ],
        compiler_params=pltpu.CompilerParams(vmem_limit_bytes=56 * 1024 * 1024),
        cost_estimate=pl.CostEstimate(
            flops=flops, transcendentals=rows * keys * heads, bytes_accessed=io_bytes
        ),
    )(q2d, k_all, v_all, do2d, lower)


def rope_tables(positions, head_width):
    half_width = head_width // 2
    indices = jnp.arange(half_width, dtype=jnp.float32)
    frequency = jnp.power(rope_base, -2.0 * indices / head_width)
    angles = positions.astype(jnp.float32)[:, None] * frequency[None, :]
    return (jnp.cos(angles)[:, None, :], jnp.sin(angles)[:, None, :])


def rotate(vector, cosine_table, sine_table):
    half_width = vector.shape[-1] // 2
    lower_half = vector[..., :half_width]
    upper_half = vector[..., half_width:]
    return jnp.concatenate(
        [
            lower_half * cosine_table - upper_half * sine_table,
            upper_half * cosine_table + lower_half * sine_table,
        ],
        axis=-1,
    )


def unrotate(rotated, cosine_table, sine_table):
    half_width = rotated.shape[-1] // 2
    lower_half = rotated[..., :half_width]
    upper_half = rotated[..., half_width:]
    return jnp.concatenate(
        [
            lower_half * cosine_table + upper_half * sine_table,
            upper_half * cosine_table - lower_half * sine_table,
        ],
        axis=-1,
    )


def normalize(vector, gain_vector):
    inv_rms = lax.rsqrt(jnp.mean(vector * vector, axis=-1, keepdims=True) + norm_eps)
    return (vector * inv_rms * gain_vector, inv_rms)


def norm_back(vector, inv_rms, gain_vector, upstream):
    scaled = upstream * gain_vector
    return inv_rms * scaled - vector * (inv_rms * inv_rms * inv_rms) * jnp.mean(
        vector * scaled, axis=-1, keepdims=True
    )


def on_device(tokens, w_query, w_key, w_value, query_gain, key_gain, positions, out_grad):
    gathered = lax.all_gather(tokens, "head", axis=0, tiled=True)
    row_count = gathered.shape[0]
    head_width = query_gain.shape[0]
    head_count = w_query.shape[1] // head_width
    groups = w_key.shape[1] // head_width
    group_size = head_count // groups
    rank_count = lax.axis_size("ctx")
    my_rank = lax.axis_index("ctx")
    reach_blocks = min((WINDOW - 2) // row_count + 1, rank_count - 1)
    core = my_rank % CORES
    partner = [(rank, rank ^ 1) for rank in range(rank_count)]
    my_rows = pair_rows(gathered, core, rank_count)
    partner_rows = lax.ppermute(
        pair_rows(gathered, CORES - 1 - core, rank_count), "ctx", partner
    )
    query_scale = 1.0 / math.sqrt(head_width)
    query_raw = jnp.dot(gathered, w_query, preferred_element_type=jnp.float32).reshape(
        row_count, head_count, head_width
    )
    key_raw = jnp.dot(gathered, w_key, preferred_element_type=jnp.float32).reshape(
        row_count, groups, head_width
    )
    value_states = jnp.dot(gathered, w_value, preferred_element_type=jnp.float32).astype(
        jnp.bfloat16
    )
    cosine_table, sine_table = rope_tables(positions, head_width)
    query_normed, query_inv = normalize(query_raw, query_gain)
    key_normed, key_inv = normalize(key_raw, key_gain)
    query_states = (
        (rotate(query_normed, cosine_table, sine_table) * query_scale)
        .astype(jnp.bfloat16)
        .reshape(row_count, groups, group_size, head_width)
    )
    key_states = (
        rotate(key_normed, cosine_table, sine_table)
        .astype(jnp.bfloat16)
        .reshape(row_count, groups * head_width)
    )
    local_kv = jnp.stack([key_states, value_states])
    blocks = [local_kv] + [
        passed_along(local_kv, "ctx", stride) for stride in range(1, reach_blocks + 1)
    ]
    offsets = jnp.arange(row_count, dtype=jnp.int32)
    key_count = (reach_blocks + 1) * row_count
    lower = jnp.maximum(
        (reach_blocks - my_rank) * row_count,
        reach_blocks * row_count + offsets - jnp.minimum(positions, WINDOW - 1),
    )[:, None]
    ordered = blocks[::-1]
    all_keys = jnp.concatenate([block[0] for block in ordered], axis=0)
    all_values = jnp.concatenate([block[1] for block in ordered], axis=0)
    attended, query_grads, key_grad_all, value_grad_all = fused_attention(
        query_states.reshape(row_count, head_count * head_width),
        all_keys,
        all_values,
        out_grad,
        lower,
        groups,
    )

    def grad_rows(stride):
        start = key_count - (stride + 1) * row_count
        return jnp.stack(
            [
                key_grad_all[start : start + row_count],
                value_grad_all[start : start + row_count],
            ]
        )

    key_grad_parts = [grad_rows(stride) for stride in range(reach_blocks + 1)]
    returned = reduce(
        jnp.add,
        [key_grad_parts[0].astype(jnp.float32)]
        + [
            passed_along(key_grad_parts[stride].astype(jnp.bfloat16), "ctx", -stride).astype(
                jnp.float32
            )
            for stride in range(1, reach_blocks + 1)
        ],
    )
    key_grads = returned[0].reshape(row_count, groups, head_width)
    value_grads = returned[1].astype(jnp.bfloat16)
    query_raw_grad = (
        norm_back(
            query_raw,
            query_inv,
            query_gain,
            unrotate(
                query_grads.reshape(row_count, head_count, head_width), cosine_table, sine_table
            )
            * query_scale,
        )
        .astype(jnp.bfloat16)
        .reshape(row_count, head_count * head_width)
    )
    key_raw_grad = (
        norm_back(key_raw, key_inv, key_gain, unrotate(key_grads, cosine_table, sine_table))
        .astype(jnp.bfloat16)
        .reshape(row_count, groups * head_width)
    )
    grad_columns = jnp.concatenate([query_raw_grad, key_raw_grad, value_grads], axis=1)
    partner_columns = lax.ppermute(grad_columns, "ctx", partner)
    pair_sum = (
        rounded_term(my_rows, grad_columns) + rounded_term(partner_rows, partner_columns)
    ).astype(jnp.bfloat16)
    pair_sum, query_raw_grad, key_raw_grad, value_grads = lax.optimization_barrier(
        (pair_sum, query_raw_grad, key_raw_grad, value_grads)
    )
    summed = torus_reduce_scatter(pair_sum, my_rank, rank_count).astype(jnp.bfloat16)
    input_terms = (
        jnp.dot(query_raw_grad, w_query.T, preferred_element_type=jnp.float32)
        + jnp.dot(key_raw_grad, w_key.T, preferred_element_type=jnp.float32)
        + jnp.dot(value_grads, w_value.T, preferred_element_type=jnp.float32)
    )
    input_grad = lax.psum_scatter(
        input_terms.astype(jnp.bfloat16), "head", scatter_dimension=0, tiled=True
    )
    query_cols = head_count * head_width
    key_cols = groups * head_width
    return (
        attended.reshape(row_count, query_cols),
        input_grad,
        summed[:, :query_cols],
        summed[:, query_cols : query_cols + key_cols],
        summed[:, query_cols + key_cols :],
    )


def solution(mesh):
    in_specs = (
        P(("ctx", "head"), None),
        P(None, "head"),
        P(None, "head"),
        P(None, "head"),
        P(),
        P(),
        P("ctx"),
        P("ctx", "head"),
    )
    out_specs = (
        P("ctx", "head"),
        P(("ctx", "head"), None),
        P("ctx", "head"),
        P("ctx", "head"),
        P("ctx", "head"),
    )
    return jax.shard_map(
        on_device, mesh=mesh, in_specs=in_specs, out_specs=out_specs, check_vma=False
    )
```
